32 devices in a mesh: corr: 2 (over x), tx: 8 (over z, core), ty: 2 (over y).
Axes of the slice: x: 2, y: 2, z: 4, core: 2. Of those that a mesh axis runs over, the one named last changes fastest.
Arguments:
- fields: float32 [2, 256, 64, 128], P(None, 'tx', 'ty'), may hold values from 0.5 to 3.5
- wind: float32 [2, 256, 64, 128], P(None, 'tx', 'ty'), may hold values from -4 to 4
- diffusion: float32 [2, 128], replicated, may hold values from 0.5 to 20
Outputs:
- levels: float32 [2, 2, 256, 64, 128], P('corr', None, 'tx', 'ty')
The draws below stay inside these ranges and needn't reach their ends.
All inputs are finite; a program needn't handle non-finite values.
Results may differ from the reference program's by a relative error of at most 0.0003.
Values sent between devices are 32-bit elements; how exact they have to be, the bound alone decides.
No kernel may reach another device: no remote copies, remote signals or barrier semaphores. Data moves between devices by JAX's collectives and lax.ppermute only.
A program may use at most 64 MiB of HBM per device.

```python
import math
import jax
import jax.numpy as jnp
import numpy as np
from jax import lax

NZ = 128
STEPS = 8
NX = 256
NY = 64
N_CORR = 2


def shard_levels(own_key, dims, shards, least, largest):
    loudness, own = 1.0, jax.random.fold_in(own_key, 6)
    for dim, blocks in shards:
        heights = jnp.exp(jax.random.uniform(jax.random.fold_in(own, dim), (blocks,), jnp.float32, least / len(shards), largest / len(shards)))
        loudness = loudness * jnp.repeat(heights, dims[dim] // blocks).reshape([-1 if axis == dim else 1 for axis in range(len(dims))])
    return loudness


def bell_draw(key, dims, scale, reach, shards=(), kind=jnp.bfloat16):
    entries = jax.random.normal(key, dims, jnp.float32) * scale
    if len(shards) > 0:
        entries = shard_levels(key, dims, shards, -0.22, 0.18) * entries
    return jnp.clip(entries, min=-reach, max=reach).astype(kind)


def setup_inputs(seed: int = 0) -> dict:
    arg_keys = jax.random.split(jax.random.key(seed), 4)
    fields = jnp.clip(0.5 + 3.0 * jax.random.uniform(arg_keys[0], (2, NX, NY, NZ), jnp.float32) ** shard_levels(arg_keys[0], (2, NX, NY, NZ), ((1, 8), (2, 2)), -0.2, 0.2), 0.5, 3.5)
    wind = bell_draw(arg_keys[1], (2, NX, NY, NZ), 1.0, 4.0, ((1, 8), (2, 2)), jnp.float32)
    diffusion = jnp.clip(jnp.exp(jax.random.uniform(arg_keys[2], (2, NZ), jnp.float32, math.log(0.5), math.log(20.0))), 0.5, 20.0)
    return dict(fields=fields, wind=wind, diffusion=diffusion)


DT = 0.1
A_RATE = 1.0
B_RATE = 3.0

def quad_cycle(count):
    table = np.zeros((count, 5))
    for m in range(count):
        first = max(0, m - 3)
        nodes = [float(j - m) for j in range(first, m + 2)]
        for i, xi in enumerate(nodes):
            coeffs = [1.0]
            for xo in nodes:
                if xo != xi:
                    widened = [0.0] * (len(coeffs) + 1)
                    for k, c in enumerate(coeffs):
                        widened[k] = widened[k] - xo * c / (xi - xo)
                        widened[k + 1] = widened[k + 1] + c / (xi - xo)
                    coeffs = widened
            integral = 0.0
            for k, c in enumerate(coeffs):
                integral = integral + c / (k + 1)
            table[m, first + i - (m - 3)] = integral
    return table

def vertical(diffusion):
    depth = diffusion.shape[1]
    keep = (jnp.arange(depth) < depth - 1).astype(jnp.float32)
    upper = diffusion * keep[None, :]
    lower = jnp.concatenate([jnp.zeros((2, 1), jnp.float32), upper[:, :-1]], 1)
    rows = jnp.arange(depth)[:, None]
    cols = jnp.arange(depth)[None, :]
    eye = (rows == cols).astype(jnp.float32)
    above = (cols == rows + 1).astype(jnp.float32)
    below = (rows == cols + 1).astype(jnp.float32)
    matrix = eye[None] + eye[None] * (lower + upper)[:, :, None] - above[None] * upper[:, :, None] - below[None] * upper[:, None, :]
    factor = jnp.linalg.cholesky(matrix)
    inverse = jax.vmap(lambda f: jax.scipy.linalg.cho_solve((f, True), eye))(factor)
    return (inverse, upper, lower)

def vertical_apply(w, upper, lower):
    zero_col = jnp.zeros(w.shape[:-1] + (1,), jnp.float32)
    beneath = jnp.concatenate([zero_col, w[..., :-1]], -1)
    overhead = jnp.concatenate([w[..., 1:], zero_col], -1)
    lo = lower[:, None, None, :]
    up = upper[:, None, None, :]
    return (lo + up) * w - lo * beneath - up * overhead

def tendency(padded, wind):
    center = padded[:, 2:-2, 2:-2]
    dx1 = (-padded[:, 4:, 2:-2] + 8.0 * padded[:, 3:-1, 2:-2] - 8.0 * padded[:, 1:-3, 2:-2] + padded[:, :-4, 2:-2]) / 12.0
    dx2 = (-padded[:, 4:, 2:-2] + 16.0 * padded[:, 3:-1, 2:-2] - 30.0 * center + 16.0 * padded[:, 1:-3, 2:-2] - padded[:, :-4, 2:-2]) / 12.0
    dy1 = (-padded[:, 2:-2, 4:] + 8.0 * padded[:, 2:-2, 3:-1] - 8.0 * padded[:, 2:-2, 1:-3] + padded[:, 2:-2, :-4]) / 12.0
    dy2 = (-padded[:, 2:-2, 4:] + 16.0 * padded[:, 2:-2, 3:-1] - 30.0 * center + 16.0 * padded[:, 2:-2, 1:-3] - padded[:, 2:-2, :-4]) / 12.0
    kappa = jnp.array([0.5, 1.0], jnp.float32)[:, None, None, None]
    first = center[0]
    second = center[1]
    square_term = first * first * second
    react = jnp.stack([A_RATE - (B_RATE + 1.0) * first + square_term, B_RATE * first - square_term], 0)
    return -(wind[0][None] * dx1 + wind[1][None] * dy1) + kappa * (dx2 + dy2) + react

def column_solve(rhs, inverse):
    return jnp.einsum('sxyk,sjk->sxyj', rhs, inverse, precision=lax.Precision.HIGHEST)

def explicit_term(state, wind):
    padded = jnp.pad(state, ((0, 0), (2, 2), (2, 2), (0, 0)), mode='wrap')
    return DT * tendency(padded, wind)

def reference(fields, wind, diffusion):
    inverse, upper, lower = vertical(diffusion)
    table = quad_cycle(STEPS)
    previous = None
    finals = []
    for level in range(N_CORR):
        state = fields
        e_list = [explicit_term(state, wind)]
        g_list = [vertical_apply(state, upper, lower)]
        for m in range(STEPS):
            rhs = state + e_list[m]
            if previous is not None:
                prev_e, prev_g = previous
                quad = jnp.zeros_like(state)
                for slot in range(5):
                    node = m - 3 + slot
                    if node >= 0:
                        quad = quad + float(table[m, slot]) * (prev_e[node] - prev_g[node])
                rhs = rhs + (quad + prev_g[m + 1] - prev_e[m])
            state = column_solve(rhs, inverse)
            e_list.append(explicit_term(state, wind))
            g_list.append(vertical_apply(state, upper, lower))
        finals.append(state)
        previous = (e_list, g_list)
    return jnp.stack(finals, 0)
```

```python
import jax
import jax.numpy as jnp
import numpy as np
from jax import lax
from jax.sharding import PartitionSpec as P

STEPS = 8


DT = 0.1
A_RATE = 1.0
B_RATE = 3.0


def quad_cycle(count):
    table = np.zeros((count, 5))
    for m in range(count):
        first = max(0, m - 3)
        nodes = [float(j - m) for j in range(first, m + 2)]
        for i, xi in enumerate(nodes):
            coeffs = [1.0]
            for xo in nodes:
                if xo != xi:
                    widened = [0.0] * (len(coeffs) + 1)
                    for k, c in enumerate(coeffs):
                        widened[k] = widened[k] - xo * c / (xi - xo)
                        widened[k + 1] = widened[k + 1] + c / (xi - xo)
                    coeffs = widened
            integral = 0.0
            for k, c in enumerate(coeffs):
                integral = integral + c / (k + 1)
            table[m, first + i - (m - 3)] = integral
    return table


def vertical(diffusion):
    depth = diffusion.shape[1]
    keep = (jnp.arange(depth) < depth - 1).astype(jnp.float32)
    upper = diffusion * keep[None, :]
    lower = jnp.concatenate([jnp.zeros((2, 1), jnp.float32), upper[:, :-1]], 1)
    rows = jnp.arange(depth)[:, None]
    cols = jnp.arange(depth)[None, :]
    eye = (rows == cols).astype(jnp.float32)
    above = (cols == rows + 1).astype(jnp.float32)
    below = (rows == cols + 1).astype(jnp.float32)
    matrix = (
        eye[None]
        + eye[None] * (lower + upper)[:, :, None]
        - above[None] * upper[:, :, None]
        - below[None] * upper[:, None, :]
    )
    factor = jnp.linalg.cholesky(matrix)
    inverse = jax.vmap(lambda f: jax.scipy.linalg.cho_solve((f, True), eye))(factor)
    return (inverse, upper, lower)


def vertical_apply(w, upper, lower):
    zero_col = jnp.zeros(w.shape[:-1] + (1,), jnp.float32)
    beneath = jnp.concatenate([zero_col, w[..., :-1]], -1)
    overhead = jnp.concatenate([w[..., 1:], zero_col], -1)
    lo = lower[:, None, None, :]
    up = upper[:, None, None, :]
    return (lo + up) * w - lo * beneath - up * overhead


def ring_halo(block, axes, dim, width):
    sizes = [lax.axis_size(axis) for axis in axes]
    size = int(np.prod(sizes))

    def mesh_index(ring_pos):
        idx = []
        for n in sizes:
            idx.append(ring_pos % n)
            ring_pos //= n
        lin = 0
        for d, n in zip(idx, sizes):
            lin = lin * n + d
        return lin

    length = block.shape[dim]
    up = [(mesh_index(g), mesh_index((g + 1) % size)) for g in range(size)]
    down = [(j, i) for i, j in up]
    last = lax.slice_in_dim(block, length - width, length, axis=dim)
    first = lax.slice_in_dim(block, 0, width, axis=dim)
    before = lax.ppermute(last, axes, up)
    after = lax.ppermute(first, axes, down)
    return before, after


def tendency(state, wind):
    west, east = ring_halo(state, ("corr", "tx"), 2, 2)
    south, north = ring_halo(state, ("ty",), 3, 2)
    px = jnp.concatenate([west, state, east], 2)
    py = jnp.concatenate([south, state, north], 3)
    center = state
    dx1 = (
        -px[:, :, 4:] + 8.0 * px[:, :, 3:-1] - 8.0 * px[:, :, 1:-3] + px[:, :, :-4]
    ) / 12.0
    dx2 = (
        -px[:, :, 4:]
        + 16.0 * px[:, :, 3:-1]
        - 30.0 * center
        + 16.0 * px[:, :, 1:-3]
        - px[:, :, :-4]
    ) / 12.0
    dy1 = (
        -py[:, :, :, 4:]
        + 8.0 * py[:, :, :, 3:-1]
        - 8.0 * py[:, :, :, 1:-3]
        + py[:, :, :, :-4]
    ) / 12.0
    dy2 = (
        -py[:, :, :, 4:]
        + 16.0 * py[:, :, :, 3:-1]
        - 30.0 * center
        + 16.0 * py[:, :, :, 1:-3]
        - py[:, :, :, :-4]
    ) / 12.0
    kappa = jnp.array([0.5, 1.0], jnp.float32)[None, :, None, None, None]
    first = center[:, 0]
    second = center[:, 1]
    square_term = first * first * second
    react = jnp.stack(
        [A_RATE - (B_RATE + 1.0) * first + square_term, B_RATE * first - square_term], 1
    )
    flow = -(wind[0][None, None] * dx1 + wind[1][None, None] * dy1)
    return DT * (flow + kappa * (dx2 + dy2) + react)


def column_solve(rhs, inverse):
    return jnp.einsum(
        "lsxyk,sjk->lsxyj", rhs, inverse, precision=lax.Precision.HIGHEST
    )


def on_device(fields, wind, diffusion):
    inverse, upper, lower = vertical(diffusion)
    table = quad_cycle(STEPS)
    depth = lax.axis_size("corr")
    slab = fields.shape[1] // depth
    start = lax.axis_index("corr") * slab
    own_fields = lax.dynamic_slice_in_dim(fields, start, slab, 1)
    own_wind = lax.dynamic_slice_in_dim(wind, start, slab, 1)

    states = [own_fields] * depth
    e_hist = [dict() for _ in range(depth)]
    d_hist = [dict() for _ in range(depth)]
    g_now = [None] * depth
    for k in range(STEPS + depth - 1):
        active = [
            l for l in range(depth)
            if 0 <= k - l < STEPS or (k - l == STEPS and l < depth - 1)
        ]
        stacked = jnp.stack([states[l] for l in active], 0)
        own_e = tendency(stacked, own_wind)
        feeds = [l for l in active if l < depth - 1]
        if feeds:
            lows = [active.index(l) for l in feeds]
            lo, hi = lows[0], lows[-1] + 1
            own_g = vertical_apply(stacked[lo:hi], upper, lower)
            for i, l in enumerate(feeds):
                m = k - l
                g_now[l] = own_g[i]
                d_hist[l][m] = own_e[lo + i] - own_g[i]
        moving = [l for l in active if k - l < STEPS]
        rhs = []
        for l in moving:
            m = k - l
            i = active.index(l)
            e_hist[l][m] = own_e[i]
            total = states[l] + own_e[i]
            if l > 0:
                quad = None
                for slot in range(5):
                    node = m - 3 + slot
                    if node >= 0:
                        term = float(table[m, slot]) * d_hist[l - 1][node]
                        quad = term if quad is None else quad + term
                total = total + (quad + g_now[l - 1] - e_hist[l - 1][m])
            rhs.append(total)
        solved = column_solve(jnp.stack(rhs, 0), inverse)
        for i, l in enumerate(moving):
            states[l] = solved[i]
    me = lax.axis_index("corr")
    result = jnp.stack(states, 0)
    out = jnp.zeros((1,) + own_fields.shape[:1] + fields.shape[1:], jnp.float32)
    out = lax.dynamic_update_slice_in_dim(
        out, lax.dynamic_index_in_dim(result, me, 0), start, 2
    )
    for shift in range(1, depth):
        pairs = [(c, (c + shift) % depth) for c in range(depth)]
        sent = lax.dynamic_index_in_dim(result, (me + shift) % depth, 0)
        got = lax.ppermute(sent, "corr", pairs)
        origin = (me - shift) % depth
        out = lax.dynamic_update_slice_in_dim(out, got, origin * slab, 2)
    return out


def solution(mesh):
    placed = (P(None, "tx", "ty", None), P(None, "tx", "ty", None), P())
    return jax.shard_map(
        on_device,
        mesh=mesh,
        in_specs=placed,
        out_specs=P("corr", None, "tx", "ty", None),
        check_vma=False,
    )
```

```python
import jax
import jax.numpy as jnp
import numpy as np
from jax import lax
from jax.experimental import pallas as pl
from jax.experimental.pallas import tpu as pltpu
from jax.sharding import PartitionSpec as P

STEPS = 8


DT = 0.1
A_RATE = 1.0
B_RATE = 3.0


def quad_cycle(count):
    table = np.zeros((count, 5))
    for m in range(count):
        first = max(0, m - 3)
        nodes = [float(j - m) for j in range(first, m + 2)]
        for i, xi in enumerate(nodes):
            coeffs = [1.0]
            for xo in nodes:
                if xo != xi:
                    widened = [0.0] * (len(coeffs) + 1)
                    for k, c in enumerate(coeffs):
                        widened[k] = widened[k] - xo * c / (xi - xo)
                        widened[k + 1] = widened[k + 1] + c / (xi - xo)
                    coeffs = widened
            integral = 0.0
            for k, c in enumerate(coeffs):
                integral = integral + c / (k + 1)
            table[m, first + i - (m - 3)] = integral
    return table


def thomas_kernel(diag_ref, up_ref, low_ref, out_ref, c_ref, d_ref):
    n = diag_ref.shape[0]
    lanes = lax.broadcasted_iota(jnp.int32, diag_ref.shape[1:], 1)
    zero = jnp.zeros(diag_ref.shape[1:], jnp.float32)

    def forward(j, carry):
        cprev, dprev = carry
        low = low_ref[j]
        inv = 1.0 / (diag_ref[j] + low * cprev)
        c = -up_ref[j] * inv
        d = (jnp.where(lanes == j, 1.0, 0.0) + low * dprev) * inv
        c_ref[j] = c
        d_ref[j] = d
        return c, d

    lax.fori_loop(0, n, forward, (zero, zero))

    def backward(i, x):
        j = n - 1 - i
        x = d_ref[j] - c_ref[j] * x
        out_ref[j] = x
        return x

    lax.fori_loop(0, n, backward, zero)


def vertical(diffusion):
    species, depth = diffusion.shape
    keep = (jnp.arange(depth) < depth - 1).astype(jnp.float32)
    upper = diffusion * keep[None, :]
    lower = jnp.concatenate([jnp.zeros((species, 1), jnp.float32), upper[:, :-1]], 1)

    def table(v):
        return jnp.broadcast_to(v.T[:, :, None], (depth, species, depth))

    rows = pl.pallas_call(
        thomas_kernel,
        out_shape=jax.ShapeDtypeStruct((depth, species, depth), jnp.float32),
        scratch_shapes=[pltpu.VMEM((depth, species, depth), jnp.float32)] * 2,
        cost_estimate=pl.CostEstimate(
            flops=12 * depth * species * depth,
            transcendentals=0,
            bytes_accessed=4 * 4 * depth * species * depth,
        ),
    )(table(1.0 + lower + upper), table(upper), table(lower))
    inverse = jnp.transpose(rows, (1, 0, 2))
    return (inverse, upper, lower)


def vertical_apply(w, upper, lower):
    zero_col = jnp.zeros(w.shape[:-1] + (1,), jnp.float32)
    beneath = jnp.concatenate([zero_col, w[..., :-1]], -1)
    overhead = jnp.concatenate([w[..., 1:], zero_col], -1)
    lo = lower[:, None, None, :]
    up = upper[:, None, None, :]
    return (lo + up) * w - lo * beneath - up * overhead


def ring_halo(block, axes, dim, width):
    sizes = [lax.axis_size(axis) for axis in axes]
    size = int(np.prod(sizes))

    def mesh_index(ring_pos):
        idx = []
        for n in sizes:
            idx.append(ring_pos % n)
            ring_pos //= n
        lin = 0
        for d, n in zip(idx, sizes):
            lin = lin * n + d
        return lin

    length = block.shape[dim]
    up = [(mesh_index(g), mesh_index((g + 1) % size)) for g in range(size)]
    down = [(j, i) for i, j in up]
    last = lax.slice_in_dim(block, length - width, length, axis=dim)
    first = lax.slice_in_dim(block, 0, width, axis=dim)
    before = lax.ppermute(last, axes, up)
    after = lax.ppermute(first, axes, down)
    return before, after


def tendency(state, wind):
    west, east = ring_halo(state, ("corr", "tx"), 2, 2)
    south, north = ring_halo(state, ("ty",), 3, 2)
    px = jnp.concatenate([west, state, east], 2)
    py = jnp.concatenate([south, state, north], 3)
    center = state
    dx1 = (
        -px[:, :, 4:] + 8.0 * px[:, :, 3:-1] - 8.0 * px[:, :, 1:-3] + px[:, :, :-4]
    ) / 12.0
    dx2 = (
        -px[:, :, 4:]
        + 16.0 * px[:, :, 3:-1]
        - 30.0 * center
        + 16.0 * px[:, :, 1:-3]
        - px[:, :, :-4]
    ) / 12.0
    dy1 = (
        -py[:, :, :, 4:]
        + 8.0 * py[:, :, :, 3:-1]
        - 8.0 * py[:, :, :, 1:-3]
        + py[:, :, :, :-4]
    ) / 12.0
    dy2 = (
        -py[:, :, :, 4:]
        + 16.0 * py[:, :, :, 3:-1]
        - 30.0 * center
        + 16.0 * py[:, :, :, 1:-3]
        - py[:, :, :, :-4]
    ) / 12.0
    kappa = jnp.array([0.5, 1.0], jnp.float32)[None, :, None, None, None]
    first = center[:, 0]
    second = center[:, 1]
    square_term = first * first * second
    react = jnp.stack(
        [A_RATE - (B_RATE + 1.0) * first + square_term, B_RATE * first - square_term], 1
    )
    flow = -(wind[0][None, None] * dx1 + wind[1][None, None] * dy1)
    return DT * (flow + kappa * (dx2 + dy2) + react)


def column_solve(rhs, inverse):
    return jnp.einsum(
        "lsxyk,sjk->lsxyj", rhs, inverse, precision=lax.Precision.HIGHEST
    )


def on_device(fields, wind, diffusion):
    inverse, upper, lower = vertical(diffusion)
    table = quad_cycle(STEPS)
    depth = lax.axis_size("corr")
    slab = fields.shape[1] // depth
    start = lax.axis_index("corr") * slab
    own_fields = lax.dynamic_slice_in_dim(fields, start, slab, 1)
    own_wind = lax.dynamic_slice_in_dim(wind, start, slab, 1)

    states = [own_fields] * depth
    e_hist = [dict() for _ in range(depth)]
    d_hist = [dict() for _ in range(depth)]
    g_now = [None] * depth
    for k in range(STEPS + depth - 1):
        active = [
            l for l in range(depth)
            if 0 <= k - l < STEPS or (k - l == STEPS and l < depth - 1)
        ]
        stacked = jnp.stack([states[l] for l in active], 0)
        own_e = tendency(stacked, own_wind)
        feeds = [l for l in active if l < depth - 1]
        if feeds:
            lows = [active.index(l) for l in feeds]
            lo, hi = lows[0], lows[-1] + 1
            own_g = vertical_apply(stacked[lo:hi], upper, lower)
            for i, l in enumerate(feeds):
                m = k - l
                g_now[l] = own_g[i]
                d_hist[l][m] = own_e[lo + i] - own_g[i]
        moving = [l for l in active if k - l < STEPS]
        rhs = []
        for l in moving:
            m = k - l
            i = active.index(l)
            e_hist[l][m] = own_e[i]
            total = states[l] + own_e[i]
            if l > 0:
                quad = None
                for slot in range(5):
                    node = m - 3 + slot
                    if node >= 0:
                        term = float(table[m, slot]) * d_hist[l - 1][node]
                        quad = term if quad is None else quad + term
                total = total + (quad + g_now[l - 1] - e_hist[l - 1][m])
            rhs.append(total)
        solved = column_solve(jnp.stack(rhs, 0), inverse)
        for i, l in enumerate(moving):
            states[l] = solved[i]
    me = lax.axis_index("corr")
    result = jnp.stack(states, 0)
    out = jnp.zeros((1,) + own_fields.shape[:1] + fields.shape[1:], jnp.float32)
    out = lax.dynamic_update_slice_in_dim(
        out, lax.dynamic_index_in_dim(result, me, 0), start, 2
    )
    for shift in range(1, depth):
        pairs = [(c, (c + shift) % depth) for c in range(depth)]
        sent = lax.dynamic_index_in_dim(result, (me + shift) % depth, 0)
        got = lax.ppermute(sent, "corr", pairs)
        origin = (me - shift) % depth
        out = lax.dynamic_update_slice_in_dim(out, got, origin * slab, 2)
    return out


def solution(mesh):
    placed = (P(None, "tx", "ty", None), P(None, "tx", "ty", None), P())
    return jax.shard_map(
        on_device,
        mesh=mesh,
        in_specs=placed,
        out_specs=P("corr", None, "tx", "ty", None),
        check_vma=False,
    )
```

```python
import jax
import jax.numpy as jnp
import numpy as np
from jax import lax
from jax.experimental import pallas as pl
from jax.experimental.pallas import tpu as pltpu
from jax.sharding import PartitionSpec as P

STEPS = 8


DT = 0.1
A_RATE = 1.0
B_RATE = 3.0


def quad_cycle(count):
    table = np.zeros((count, 5))
    for m in range(count):
        first = max(0, m - 3)
        nodes = [float(j - m) for j in range(first, m + 2)]
        for i, xi in enumerate(nodes):
            coeffs = [1.0]
            for xo in nodes:
                if xo != xi:
                    widened = [0.0] * (len(coeffs) + 1)
                    for k, c in enumerate(coeffs):
                        widened[k] = widened[k] - xo * c / (xi - xo)
                        widened[k + 1] = widened[k + 1] + c / (xi - xo)
                    coeffs = widened
            integral = 0.0
            for k, c in enumerate(coeffs):
                integral = integral + c / (k + 1)
            table[m, first + i - (m - 3)] = integral
    return table


def thomas_kernel(up_ref, low_ref, out_ref, c_ref, d_ref):
    n = out_ref.shape[0]
    shape = out_ref.shape[1:]
    lanes = lax.broadcasted_iota(jnp.int32, shape, 1)
    species = lax.broadcasted_iota(jnp.int32, shape, 0)
    zero = jnp.zeros(shape, jnp.float32)

    def column(ref, j):
        value = jnp.full(shape, ref[0, j], jnp.float32)
        for s in range(1, shape[0]):
            value = jnp.where(species == s, ref[s, j], value)
        return value

    def forward(j, carry):
        cprev, dprev = carry
        up = column(up_ref, j)
        low = column(low_ref, j)
        inv = 1.0 / ((1.0 + low + up) + low * cprev)
        c = -up * inv
        d = (jnp.where(lanes == j, 1.0, 0.0) + low * dprev) * inv
        c_ref[j] = c
        d_ref[j] = d
        return c, d

    lax.fori_loop(0, n, forward, (zero, zero))

    def backward(i, x):
        j = n - 1 - i
        x = d_ref[j] - c_ref[j] * x
        out_ref[j] = x
        return x

    lax.fori_loop(0, n, backward, zero)


def vertical(diffusion):
    species, depth = diffusion.shape
    keep = (jnp.arange(depth) < depth - 1).astype(jnp.float32)
    upper = diffusion * keep[None, :]
    lower = jnp.concatenate([jnp.zeros((species, 1), jnp.float32), upper[:, :-1]], 1)
    rows = pl.pallas_call(
        thomas_kernel,
        out_shape=jax.ShapeDtypeStruct((depth, species, depth), jnp.float32),
        in_specs=[pl.BlockSpec(memory_space=pltpu.SMEM)] * 2,
        scratch_shapes=[pltpu.VMEM((depth, species, depth), jnp.float32)] * 2,
        cost_estimate=pl.CostEstimate(
            flops=12 * depth * species * depth,
            transcendentals=0,
            bytes_accessed=4 * 2 * depth * species * depth,
        ),
    )(upper, lower)
    inverse = jnp.transpose(rows, (1, 0, 2))
    return (inverse, upper, lower)


def vertical_apply(w, upper, lower):
    zero_col = jnp.zeros(w.shape[:-1] + (1,), jnp.float32)
    beneath = jnp.concatenate([zero_col, w[..., :-1]], -1)
    overhead = jnp.concatenate([w[..., 1:], zero_col], -1)
    lo = lower[:, None, None, :]
    up = upper[:, None, None, :]
    return (lo + up) * w - lo * beneath - up * overhead


def ring_halo(block, axes, dim, width):
    sizes = [lax.axis_size(axis) for axis in axes]
    size = int(np.prod(sizes))

    def mesh_index(ring_pos):
        idx = []
        for n in sizes:
            idx.append(ring_pos % n)
            ring_pos //= n
        lin = 0
        for d, n in zip(idx, sizes):
            lin = lin * n + d
        return lin

    length = block.shape[dim]
    up = [(mesh_index(g), mesh_index((g + 1) % size)) for g in range(size)]
    down = [(j, i) for i, j in up]
    last = lax.slice_in_dim(block, length - width, length, axis=dim)
    first = lax.slice_in_dim(block, 0, width, axis=dim)
    if size == 2:
        got = lax.ppermute(jnp.concatenate([first, last], dim), axes, up)
        after = lax.slice_in_dim(got, 0, width, axis=dim)
        before = lax.slice_in_dim(got, width, 2 * width, axis=dim)
        return before, after
    before = lax.ppermute(last, axes, up)
    after = lax.ppermute(first, axes, down)
    return before, after


def tendency(state, wind):
    west, east = ring_halo(state, ("corr", "tx"), 2, 2)
    south, north = ring_halo(state, ("ty",), 3, 2)
    px = jnp.concatenate([west, state, east], 2)
    py = jnp.concatenate([south, state, north], 3)
    center = state
    dx1 = (
        -px[:, :, 4:] + 8.0 * px[:, :, 3:-1] - 8.0 * px[:, :, 1:-3] + px[:, :, :-4]
    ) / 12.0
    dx2 = (
        -px[:, :, 4:]
        + 16.0 * px[:, :, 3:-1]
        - 30.0 * center
        + 16.0 * px[:, :, 1:-3]
        - px[:, :, :-4]
    ) / 12.0
    dy1 = (
        -py[:, :, :, 4:]
        + 8.0 * py[:, :, :, 3:-1]
        - 8.0 * py[:, :, :, 1:-3]
        + py[:, :, :, :-4]
    ) / 12.0
    dy2 = (
        -py[:, :, :, 4:]
        + 16.0 * py[:, :, :, 3:-1]
        - 30.0 * center
        + 16.0 * py[:, :, :, 1:-3]
        - py[:, :, :, :-4]
    ) / 12.0
    kappa = jnp.array([0.5, 1.0], jnp.float32)[None, :, None, None, None]
    first = center[:, 0]
    second = center[:, 1]
    square_term = first * first * second
    react = jnp.stack(
        [A_RATE - (B_RATE + 1.0) * first + square_term, B_RATE * first - square_term], 1
    )
    flow = -(wind[0][None, None] * dx1 + wind[1][None, None] * dy1)
    return DT * (flow + kappa * (dx2 + dy2) + react)


def column_solve(rhs, inverse):
    return jnp.einsum(
        "lsxyk,sjk->lsxyj", rhs, inverse, precision=lax.Precision.HIGHEST
    )


def on_device(fields, wind, diffusion):
    inverse, upper, lower = vertical(diffusion)
    table = quad_cycle(STEPS)
    depth = lax.axis_size("corr")
    slab = fields.shape[1] // depth
    start = lax.axis_index("corr") * slab
    own_fields = lax.dynamic_slice_in_dim(fields, start, slab, 1)
    own_wind = lax.dynamic_slice_in_dim(wind, start, slab, 1)

    states = [own_fields] * depth
    e_hist = [dict() for _ in range(depth)]
    d_hist = [dict() for _ in range(depth)]
    g_now = [None] * depth
    for k in range(STEPS + depth - 1):
        active = [
            l for l in range(depth)
            if 0 <= k - l < STEPS or (k - l == STEPS and l < depth - 1)
        ]
        stacked = jnp.stack([states[l] for l in active], 0)
        own_e = tendency(stacked, own_wind)
        feeds = [l for l in active if l < depth - 1]
        if feeds:
            lows = [active.index(l) for l in feeds]
            lo, hi = lows[0], lows[-1] + 1
            own_g = vertical_apply(stacked[lo:hi], upper, lower)
            for i, l in enumerate(feeds):
                m = k - l
                g_now[l] = own_g[i]
                d_hist[l][m] = own_e[lo + i] - own_g[i]
        moving = [l for l in active if k - l < STEPS]
        rhs = []
        for l in moving:
            m = k - l
            i = active.index(l)
            e_hist[l][m] = own_e[i]
            total = states[l] + own_e[i]
            if l > 0:
                quad = None
                for slot in range(5):
                    node = m - 3 + slot
                    if node >= 0:
                        term = float(table[m, slot]) * d_hist[l - 1][node]
                        quad = term if quad is None else quad + term
                total = total + (quad + g_now[l - 1] - e_hist[l - 1][m])
            rhs.append(total)
        solved = column_solve(jnp.stack(rhs, 0), inverse)
        for i, l in enumerate(moving):
            states[l] = solved[i]
    me = lax.axis_index("corr")
    result = jnp.stack(states, 0)
    out = jnp.zeros((1,) + own_fields.shape[:1] + fields.shape[1:], jnp.float32)
    out = lax.dynamic_update_slice_in_dim(
        out, lax.dynamic_index_in_dim(result, me, 0), start, 2
    )
    for shift in range(1, depth):
        pairs = [(c, (c + shift) % depth) for c in range(depth)]
        sent = lax.dynamic_index_in_dim(result, (me + shift) % depth, 0)
        got = lax.ppermute(sent, "corr", pairs)
        origin = (me - shift) % depth
        out = lax.dynamic_update_slice_in_dim(out, got, origin * slab, 2)
    return out


def solution(mesh):
    placed = (P(None, "tx", "ty", None), P(None, "tx", "ty", None), P())
    return jax.shard_map(
        on_device,
        mesh=mesh,
        in_specs=placed,
        out_specs=P("corr", None, "tx", "ty", None),
        check_vma=False,
    )
```

```python
import jax
import jax.numpy as jnp
import numpy as np
from jax import lax
from jax.experimental import pallas as pl
from jax.experimental.pallas import tpu as pltpu
from jax.sharding import PartitionSpec as P

STEPS = 8


DT = 0.1
A_RATE = 1.0
B_RATE = 3.0


def quad_cycle(count):
    table = np.zeros((count, 5))
    for m in range(count):
        first = max(0, m - 3)
        nodes = [float(j - m) for j in range(first, m + 2)]
        for i, xi in enumerate(nodes):
            coeffs = [1.0]
            for xo in nodes:
                if xo != xi:
                    widened = [0.0] * (len(coeffs) + 1)
                    for k, c in enumerate(coeffs):
                        widened[k] = widened[k] - xo * c / (xi - xo)
                        widened[k + 1] = widened[k + 1] + c / (xi - xo)
                    coeffs = widened
            integral = 0.0
            for k, c in enumerate(coeffs):
                integral = integral + c / (k + 1)
            table[m, first + i - (m - 3)] = integral
    return table


def thomas_kernel(up_ref, low_ref, out_ref, c_ref, d_ref):
    n = out_ref.shape[0]
    shape = out_ref.shape[1:]
    lanes = lax.broadcasted_iota(jnp.int32, shape, 1)
    species = lax.broadcasted_iota(jnp.int32, shape, 0)
    zero = jnp.zeros(shape, jnp.float32)

    def column(ref, j):
        value = jnp.full(shape, ref[0, j], jnp.float32)
        for s in range(1, shape[0]):
            value = jnp.where(species == s, ref[s, j], value)
        return value

    def forward(j, carry):
        cprev, dprev = carry
        up = column(up_ref, j)
        low = column(low_ref, j)
        inv = 1.0 / ((1.0 + low + up) + low * cprev)
        c = -up * inv
        d = (jnp.where(lanes == j, 1.0, 0.0) + low * dprev) * inv
        c_ref[j] = c
        d_ref[j] = d
        return c, d

    lax.fori_loop(0, n, forward, (zero, zero))

    def backward(i, x):
        j = n - 1 - i
        x = d_ref[j] - c_ref[j] * x
        out_ref[j] = x
        return x

    lax.fori_loop(0, n, backward, zero)


def vertical(diffusion):
    species, depth = diffusion.shape
    keep = (jnp.arange(depth) < depth - 1).astype(jnp.float32)
    upper = diffusion * keep[None, :]
    lower = jnp.concatenate([jnp.zeros((species, 1), jnp.float32), upper[:, :-1]], 1)
    rows = pl.pallas_call(
        thomas_kernel,
        out_shape=jax.ShapeDtypeStruct((depth, species, depth), jnp.float32),
        in_specs=[pl.BlockSpec(memory_space=pltpu.SMEM)] * 2,
        scratch_shapes=[pltpu.VMEM((depth, species, depth), jnp.float32)] * 2,
        cost_estimate=pl.CostEstimate(
            flops=12 * depth * species * depth,
            transcendentals=0,
            bytes_accessed=4 * 2 * depth * species * depth,
        ),
    )(upper, lower)
    inverse = jnp.transpose(rows, (1, 0, 2))
    return (inverse, upper, lower)


def vertical_apply(w, upper, lower):
    zero_col = jnp.zeros(w.shape[:-1] + (1,), jnp.float32)
    beneath = jnp.concatenate([zero_col, w[..., :-1]], -1)
    overhead = jnp.concatenate([w[..., 1:], zero_col], -1)
    lo = lower[:, None, None, :]
    up = upper[:, None, None, :]
    return (lo + up) * w - lo * beneath - up * overhead


def slab_of(corr, tile, depth):
    return jnp.where(tile % 2 == 0, corr, depth - 1 - corr)


def x_ring():
    depth, tiles = lax.axis_size("corr"), lax.axis_size("tx")
    order = []
    for tile in range(tiles):
        for q in range(depth):
            corr = q if tile % 2 == 0 else depth - 1 - q
            order.append(corr * tiles + tile)
    return order


def ring_halo(block, axes, order, dim, width):
    size = len(order)
    length = block.shape[dim]
    up = [(order[g], order[(g + 1) % size]) for g in range(size)]
    down = [(j, i) for i, j in up]
    last = lax.slice_in_dim(block, length - width, length, axis=dim)
    first = lax.slice_in_dim(block, 0, width, axis=dim)
    if size == 2:
        got = lax.ppermute(jnp.concatenate([first, last], dim), axes, up)
        after = lax.slice_in_dim(got, 0, width, axis=dim)
        before = lax.slice_in_dim(got, width, 2 * width, axis=dim)
        return before, after
    before = lax.ppermute(last, axes, up)
    after = lax.ppermute(first, axes, down)
    return before, after


def tendency(state, wind):
    west, east = ring_halo(state, ("corr", "tx"), x_ring(), 2, 2)
    south, north = ring_halo(state, ("ty",), list(range(lax.axis_size("ty"))), 3, 2)
    px = jnp.concatenate([west, state, east], 2)
    py = jnp.concatenate([south, state, north], 3)
    center = state
    dx1 = (
        -px[:, :, 4:] + 8.0 * px[:, :, 3:-1] - 8.0 * px[:, :, 1:-3] + px[:, :, :-4]
    ) / 12.0
    dx2 = (
        -px[:, :, 4:]
        + 16.0 * px[:, :, 3:-1]
        - 30.0 * center
        + 16.0 * px[:, :, 1:-3]
        - px[:, :, :-4]
    ) / 12.0
    dy1 = (
        -py[:, :, :, 4:]
        + 8.0 * py[:, :, :, 3:-1]
        - 8.0 * py[:, :, :, 1:-3]
        + py[:, :, :, :-4]
    ) / 12.0
    dy2 = (
        -py[:, :, :, 4:]
        + 16.0 * py[:, :, :, 3:-1]
        - 30.0 * center
        + 16.0 * py[:, :, :, 1:-3]
        - py[:, :, :, :-4]
    ) / 12.0
    kappa = jnp.array([0.5, 1.0], jnp.float32)[None, :, None, None, None]
    first = center[:, 0]
    second = center[:, 1]
    square_term = first * first * second
    react = jnp.stack(
        [A_RATE - (B_RATE + 1.0) * first + square_term, B_RATE * first - square_term], 1
    )
    flow = -(wind[0][None, None] * dx1 + wind[1][None, None] * dy1)
    return DT * (flow + kappa * (dx2 + dy2) + react)


def column_solve(rhs, inverse):
    return jnp.einsum(
        "lsxyk,sjk->lsxyj", rhs, inverse, precision=lax.Precision.HIGHEST
    )


def on_device(fields, wind, diffusion):
    inverse, upper, lower = vertical(diffusion)
    table = quad_cycle(STEPS)
    depth = lax.axis_size("corr")
    slab = fields.shape[1] // depth
    me = lax.axis_index("corr")
    tile = lax.axis_index("tx")
    start = slab_of(me, tile, depth) * slab
    own_fields = lax.dynamic_slice_in_dim(fields, start, slab, 1)
    own_wind = lax.dynamic_slice_in_dim(wind, start, slab, 1)

    states = [own_fields] * depth
    e_hist = [dict() for _ in range(depth)]
    d_hist = [dict() for _ in range(depth)]
    g_now = [None] * depth
    for k in range(STEPS + depth - 1):
        active = [
            l for l in range(depth)
            if 0 <= k - l < STEPS or (k - l == STEPS and l < depth - 1)
        ]
        stacked = jnp.stack([states[l] for l in active], 0)
        own_e = tendency(stacked, own_wind)
        feeds = [l for l in active if l < depth - 1]
        if feeds:
            lows = [active.index(l) for l in feeds]
            lo, hi = lows[0], lows[-1] + 1
            own_g = vertical_apply(stacked[lo:hi], upper, lower)
            for i, l in enumerate(feeds):
                m = k - l
                g_now[l] = own_g[i]
                d_hist[l][m] = own_e[lo + i] - own_g[i]
        moving = [l for l in active if k - l < STEPS]
        rhs = []
        for l in moving:
            m = k - l
            i = active.index(l)
            e_hist[l][m] = own_e[i]
            total = states[l] + own_e[i]
            if l > 0:
                quad = None
                for slot in range(5):
                    node = m - 3 + slot
                    if node >= 0:
                        term = float(table[m, slot]) * d_hist[l - 1][node]
                        quad = term if quad is None else quad + term
                total = total + (quad + g_now[l - 1] - e_hist[l - 1][m])
            rhs.append(total)
        solved = column_solve(jnp.stack(rhs, 0), inverse)
        for i, l in enumerate(moving):
            states[l] = solved[i]
    result = jnp.stack(states, 0)
    out = jnp.zeros((1,) + own_fields.shape[:1] + fields.shape[1:], jnp.float32)
    out = lax.dynamic_update_slice_in_dim(
        out, lax.dynamic_index_in_dim(result, me, 0), start, 2
    )
    for shift in range(1, depth):
        pairs = [(c, (c + shift) % depth) for c in range(depth)]
        sent = lax.dynamic_index_in_dim(result, (me + shift) % depth, 0)
        got = lax.ppermute(sent, "corr", pairs)
        origin = (me - shift) % depth
        out = lax.dynamic_update_slice_in_dim(
            out, got, slab_of(origin, tile, depth) * slab, 2
        )
    return out


def solution(mesh):
    placed = (P(None, "tx", "ty", None), P(None, "tx", "ty", None), P())
    return jax.shard_map(
        on_device,
        mesh=mesh,
        in_specs=placed,
        out_specs=P("corr", None, "tx", "ty", None),
        check_vma=False,
    )
```

```python
import jax
import jax.numpy as jnp
import numpy as np
from jax import lax
from jax.experimental import pallas as pl
from jax.experimental.pallas import tpu as pltpu
from jax.sharding import PartitionSpec as P

STEPS = 8


DT = 0.1
A_RATE = 1.0
B_RATE = 3.0


def quad_cycle(count):
    table = np.zeros((count, 5))
    for m in range(count):
        first = max(0, m - 3)
        nodes = [float(j - m) for j in range(first, m + 2)]
        for i, xi in enumerate(nodes):
            coeffs = [1.0]
            for xo in nodes:
                if xo != xi:
                    widened = [0.0] * (len(coeffs) + 1)
                    for k, c in enumerate(coeffs):
                        widened[k] = widened[k] - xo * c / (xi - xo)
                        widened[k + 1] = widened[k + 1] + c / (xi - xo)
                    coeffs = widened
            integral = 0.0
            for k, c in enumerate(coeffs):
                integral = integral + c / (k + 1)
            table[m, first + i - (m - 3)] = integral
    return table


def thomas_kernel(up_ref, low_ref, out_ref, c_ref, d_ref):
    n = out_ref.shape[0]
    shape = out_ref.shape[1:]
    lanes = lax.broadcasted_iota(jnp.int32, shape, 1)
    species = lax.broadcasted_iota(jnp.int32, shape, 0)
    zero = jnp.zeros(shape, jnp.float32)

    def column(ref, j):
        value = jnp.full(shape, ref[0, j], jnp.float32)
        for s in range(1, shape[0]):
            value = jnp.where(species == s, ref[s, j], value)
        return value

    def forward(j, carry):
        cprev, dprev = carry
        up = column(up_ref, j)
        low = column(low_ref, j)
        inv = 1.0 / ((1.0 + low + up) + low * cprev)
        c = -up * inv
        d = (jnp.where(lanes == j, 1.0, 0.0) + low * dprev) * inv
        c_ref[j] = c
        d_ref[j] = d
        return c, d

    lax.fori_loop(0, n, forward, (zero, zero))

    def backward(i, x):
        j = n - 1 - i
        x = d_ref[j] - c_ref[j] * x
        out_ref[j] = x
        return x

    lax.fori_loop(0, n, backward, zero)


def vertical(diffusion):
    species, depth = diffusion.shape
    keep = (jnp.arange(depth) < depth - 1).astype(jnp.float32)
    upper = diffusion * keep[None, :]
    lower = jnp.concatenate([jnp.zeros((species, 1), jnp.float32), upper[:, :-1]], 1)
    rows = pl.pallas_call(
        thomas_kernel,
        out_shape=jax.ShapeDtypeStruct((depth, species, depth), jnp.float32),
        in_specs=[pl.BlockSpec(memory_space=pltpu.SMEM)] * 2,
        scratch_shapes=[pltpu.VMEM((depth, species, depth), jnp.float32)] * 2,
        cost_estimate=pl.CostEstimate(
            flops=12 * depth * species * depth,
            transcendentals=0,
            bytes_accessed=4 * 2 * depth * species * depth,
        ),
    )(upper, lower)
    inverse = jnp.transpose(rows, (1, 0, 2))
    return (inverse, upper, lower)


def vertical_apply(w, upper, lower):
    zero_col = jnp.zeros(w.shape[:-1] + (1,), jnp.float32)
    beneath = jnp.concatenate([zero_col, w[..., :-1]], -1)
    overhead = jnp.concatenate([w[..., 1:], zero_col], -1)
    lo = lower[:, None, None, :]
    up = upper[:, None, None, :]
    return (lo + up) * w - lo * beneath - up * overhead


def slab_of(corr, tile, depth):
    return jnp.where(tile % 2 == 0, corr, depth - 1 - corr)


def x_ring():
    depth, tiles = lax.axis_size("corr"), lax.axis_size("tx")
    order = []
    for tile in range(tiles):
        for q in range(depth):
            corr = q if tile % 2 == 0 else depth - 1 - q
            order.append(corr * tiles + tile)
    return order


def ring_halo(block, axes, order, dim, width):
    size = len(order)
    length = block.shape[dim]
    up = [(order[g], order[(g + 1) % size]) for g in range(size)]
    down = [(j, i) for i, j in up]
    last = lax.slice_in_dim(block, length - width, length, axis=dim)
    first = lax.slice_in_dim(block, 0, width, axis=dim)
    if size == 2:
        got = lax.ppermute(jnp.concatenate([first, last], dim), axes, up)
        after = lax.slice_in_dim(got, 0, width, axis=dim)
        before = lax.slice_in_dim(got, width, 2 * width, axis=dim)
        return before, after
    before = lax.ppermute(last, axes, up)
    after = lax.ppermute(first, axes, down)
    return before, after


def tendency(state, wind):
    west, east = ring_halo(state, ("corr", "tx"), x_ring(), 2, 2)
    south, north = ring_halo(state, ("ty",), list(range(lax.axis_size("ty"))), 3, 2)
    px = jnp.concatenate([west, state, east], 2)
    py = jnp.concatenate([south, state, north], 3)
    center = state
    dx1 = (
        -px[:, :, 4:] + 8.0 * px[:, :, 3:-1] - 8.0 * px[:, :, 1:-3] + px[:, :, :-4]
    ) / 12.0
    dx2 = (
        -px[:, :, 4:]
        + 16.0 * px[:, :, 3:-1]
        - 30.0 * center
        + 16.0 * px[:, :, 1:-3]
        - px[:, :, :-4]
    ) / 12.0
    dy1 = (
        -py[:, :, :, 4:]
        + 8.0 * py[:, :, :, 3:-1]
        - 8.0 * py[:, :, :, 1:-3]
        + py[:, :, :, :-4]
    ) / 12.0
    dy2 = (
        -py[:, :, :, 4:]
        + 16.0 * py[:, :, :, 3:-1]
        - 30.0 * center
        + 16.0 * py[:, :, :, 1:-3]
        - py[:, :, :, :-4]
    ) / 12.0
    kappa = jnp.array([0.5, 1.0], jnp.float32)[None, :, None, None, None]
    first = center[:, 0]
    second = center[:, 1]
    square_term = first * first * second
    react = jnp.stack(
        [A_RATE - (B_RATE + 1.0) * first + square_term, B_RATE * first - square_term], 1
    )
    flow = -(wind[0][None, None] * dx1 + wind[1][None, None] * dy1)
    return DT * (flow + kappa * (dx2 + dy2) + react)


def column_solve(rhs, inverse):
    return jnp.einsum(
        "lsxyk,sjk->lsxyj", rhs, inverse, precision=lax.Precision.HIGHEST
    )


def on_device(fields, wind, diffusion):
    inverse, upper, lower = vertical(diffusion)
    table = quad_cycle(STEPS)
    depth = lax.axis_size("corr")
    slab = fields.shape[1] // depth
    me = lax.axis_index("corr")
    tile = lax.axis_index("tx")
    start = slab_of(me, tile, depth) * slab
    own_fields = lax.dynamic_slice_in_dim(fields, start, slab, 1)
    own_wind = lax.dynamic_slice_in_dim(wind, start, slab, 1)

    states = [own_fields] * depth
    e_hist = [dict() for _ in range(depth)]
    d_hist = [dict() for _ in range(depth)]
    g_now = [None] * depth
    for k in range(STEPS + depth - 1):
        active = [
            l for l in range(depth)
            if 0 <= k - l < STEPS or (k - l == STEPS and l < depth - 1)
        ]
        own_e = {}
        for l in active:
            m = k - l
            own_e[l] = tendency(states[l][None], own_wind)[0]
            if l < depth - 1:
                g_now[l] = vertical_apply(states[l][None], upper, lower)[0]
                d_hist[l][m] = own_e[l] - g_now[l]
        for l in active:
            m = k - l
            if m >= STEPS:
                continue
            e_hist[l][m] = own_e[l]
            total = states[l] + own_e[l]
            if l > 0:
                quad = None
                for slot in range(5):
                    node = m - 3 + slot
                    if node >= 0:
                        term = float(table[m, slot]) * d_hist[l - 1][node]
                        quad = term if quad is None else quad + term
                total = total + (quad + g_now[l - 1] - e_hist[l - 1][m])
            states[l] = column_solve(total[None], inverse)[0]
    result = jnp.stack(states, 0)
    out = jnp.zeros((1,) + own_fields.shape[:1] + fields.shape[1:], jnp.float32)
    out = lax.dynamic_update_slice_in_dim(
        out, lax.dynamic_index_in_dim(result, me, 0), start, 2
    )
    for shift in range(1, depth):
        pairs = [(c, (c + shift) % depth) for c in range(depth)]
        sent = lax.dynamic_index_in_dim(result, (me + shift) % depth, 0)
        got = lax.ppermute(sent, "corr", pairs)
        origin = (me - shift) % depth
        out = lax.dynamic_update_slice_in_dim(
            out, got, slab_of(origin, tile, depth) * slab, 2
        )
    return out


def solution(mesh):
    placed = (P(None, "tx", "ty", None), P(None, "tx", "ty", None), P())
    return jax.shard_map(
        on_device,
        mesh=mesh,
        in_specs=placed,
        out_specs=P("corr", None, "tx", "ty", None),
        check_vma=False,
    )
```

```python
import jax
import jax.numpy as jnp
import numpy as np
from jax import lax
from jax.experimental import pallas as pl
from jax.experimental.pallas import tpu as pltpu
from jax.sharding import PartitionSpec as P

STEPS = 8


DT = 0.1
A_RATE = 1.0
B_RATE = 3.0


def quad_cycle(count):
    table = np.zeros((count, 5))
    for m in range(count):
        first = max(0, m - 3)
        nodes = [float(j - m) for j in range(first, m + 2)]
        for i, xi in enumerate(nodes):
            coeffs = [1.0]
            for xo in nodes:
                if xo != xi:
                    widened = [0.0] * (len(coeffs) + 1)
                    for k, c in enumerate(coeffs):
                        widened[k] = widened[k] - xo * c / (xi - xo)
                        widened[k + 1] = widened[k + 1] + c / (xi - xo)
                    coeffs = widened
            integral = 0.0
            for k, c in enumerate(coeffs):
                integral = integral + c / (k + 1)
            table[m, first + i - (m - 3)] = integral
    return table


def thomas_kernel(up_ref, low_ref, out_ref, c_ref, d_ref):
    n = out_ref.shape[0]
    shape = out_ref.shape[1:]
    lanes = lax.broadcasted_iota(jnp.int32, shape, 1)
    species = lax.broadcasted_iota(jnp.int32, shape, 0)
    zero = jnp.zeros(shape, jnp.float32)

    def column(ref, j):
        value = jnp.full(shape, ref[0, j], jnp.float32)
        for s in range(1, shape[0]):
            value = jnp.where(species == s, ref[s, j], value)
        return value

    def forward(j, carry):
        cprev, dprev = carry
        up = column(up_ref, j)
        low = column(low_ref, j)
        inv = 1.0 / ((1.0 + low + up) + low * cprev)
        c = -up * inv
        d = (jnp.where(lanes == j, 1.0, 0.0) + low * dprev) * inv
        c_ref[j] = c
        d_ref[j] = d
        return c, d

    lax.fori_loop(0, n, forward, (zero, zero))

    def backward(i, x):
        j = n - 1 - i
        x = d_ref[j] - c_ref[j] * x
        out_ref[j] = x
        return x

    lax.fori_loop(0, n, backward, zero)


def vertical(diffusion):
    species, depth = diffusion.shape
    keep = (jnp.arange(depth) < depth - 1).astype(jnp.float32)
    upper = diffusion * keep[None, :]
    lower = jnp.concatenate([jnp.zeros((species, 1), jnp.float32), upper[:, :-1]], 1)
    rows = pl.pallas_call(
        thomas_kernel,
        out_shape=jax.ShapeDtypeStruct((depth, species, depth), jnp.float32),
        in_specs=[pl.BlockSpec(memory_space=pltpu.SMEM)] * 2,
        scratch_shapes=[pltpu.VMEM((depth, species, depth), jnp.float32)] * 2,
        cost_estimate=pl.CostEstimate(
            flops=12 * depth * species * depth,
            transcendentals=0,
            bytes_accessed=4 * 2 * depth * species * depth,
        ),
    )(upper, lower)
    inverse = jnp.transpose(rows, (1, 0, 2))
    return (inverse, upper, lower)


def vertical_apply(w, upper, lower):
    zero_col = jnp.zeros(w.shape[:-1] + (1,), jnp.float32)
    beneath = jnp.concatenate([zero_col, w[..., :-1]], -1)
    overhead = jnp.concatenate([w[..., 1:], zero_col], -1)
    lo = lower[:, None, None, :]
    up = upper[:, None, None, :]
    return (lo + up) * w - lo * beneath - up * overhead


def slab_of(corr, tile, depth):
    return jnp.where(tile % 2 == 0, corr, depth - 1 - corr)


def x_ring():
    depth, tiles = lax.axis_size("corr"), lax.axis_size("tx")
    order = []
    for tile in range(tiles):
        for q in range(depth):
            corr = q if tile % 2 == 0 else depth - 1 - q
            order.append(corr * tiles + tile)
    return order


def ring_halo(block, axes, order, dim, width):
    size = len(order)
    length = block.shape[dim]
    up = [(order[g], order[(g + 1) % size]) for g in range(size)]
    down = [(j, i) for i, j in up]
    last = lax.slice_in_dim(block, length - width, length, axis=dim)
    first = lax.slice_in_dim(block, 0, width, axis=dim)
    if size == 2:
        got = lax.ppermute(jnp.concatenate([first, last], dim), axes, up)
        after = lax.slice_in_dim(got, 0, width, axis=dim)
        before = lax.slice_in_dim(got, width, 2 * width, axis=dim)
        return before, after
    before = lax.ppermute(last, axes, up)
    after = lax.ppermute(first, axes, down)
    return before, after


def tendency(state, wind):
    west, east = ring_halo(state, ("corr", "tx"), x_ring(), 2, 2)
    south, north = ring_halo(state, ("ty",), list(range(lax.axis_size("ty"))), 3, 2)
    px = jnp.concatenate([west, state, east], 2)
    py = jnp.concatenate([south, state, north], 3)
    center = state
    dx1 = (
        -px[:, :, 4:] + 8.0 * px[:, :, 3:-1] - 8.0 * px[:, :, 1:-3] + px[:, :, :-4]
    ) / 12.0
    dx2 = (
        -px[:, :, 4:]
        + 16.0 * px[:, :, 3:-1]
        - 30.0 * center
        + 16.0 * px[:, :, 1:-3]
        - px[:, :, :-4]
    ) / 12.0
    dy1 = (
        -py[:, :, :, 4:]
        + 8.0 * py[:, :, :, 3:-1]
        - 8.0 * py[:, :, :, 1:-3]
        + py[:, :, :, :-4]
    ) / 12.0
    dy2 = (
        -py[:, :, :, 4:]
        + 16.0 * py[:, :, :, 3:-1]
        - 30.0 * center
        + 16.0 * py[:, :, :, 1:-3]
        - py[:, :, :, :-4]
    ) / 12.0
    kappa = jnp.array([0.5, 1.0], jnp.float32)[None, :, None, None, None]
    first = center[:, 0]
    second = center[:, 1]
    square_term = first * first * second
    react = jnp.stack(
        [A_RATE - (B_RATE + 1.0) * first + square_term, B_RATE * first - square_term], 1
    )
    flow = -(wind[0][None, None] * dx1 + wind[1][None, None] * dy1)
    return DT * (flow + kappa * (dx2 + dy2) + react)


def column_solve(rhs, inverse):
    return jnp.einsum(
        "lsxyk,sjk->lsxyj", rhs, inverse, precision=lax.Precision.HIGHEST
    )


def on_device(fields, wind, diffusion):
    inverse, upper, lower = vertical(diffusion)
    table = quad_cycle(STEPS)
    depth = lax.axis_size("corr")
    slab = fields.shape[1] // depth
    me = lax.axis_index("corr")
    tile = lax.axis_index("tx")
    start = slab_of(me, tile, depth) * slab
    own_fields = lax.dynamic_slice_in_dim(fields, start, slab, 1)
    own_wind = lax.dynamic_slice_in_dim(wind, start, slab, 1)

    states = [own_fields] * depth
    e_hist = [dict() for _ in range(depth)]
    d_hist = [dict() for _ in range(depth)]
    g_now = [None] * depth
    for k in range(STEPS + depth - 1):
        active = [
            l for l in range(depth)
            if 0 <= k - l < STEPS or (k - l == STEPS and l < depth - 1)
        ]
        stacked = jnp.stack([states[l] for l in active], 0)
        own_e = tendency(stacked, own_wind)
        feeds = [l for l in active if l < depth - 1]
        if feeds:
            lows = [active.index(l) for l in feeds]
            lo, hi = lows[0], lows[-1] + 1
            own_g = vertical_apply(stacked[lo:hi], upper, lower)
            for i, l in enumerate(feeds):
                m = k - l
                g_now[l] = own_g[i]
                d_hist[l][m] = own_e[lo + i] - own_g[i]
        moving = [l for l in active if k - l < STEPS]
        rhs = []
        for l in moving:
            m = k - l
            i = active.index(l)
            e_hist[l][m] = own_e[i]
            total = states[l] + own_e[i]
            if l > 0:
                quad = None
                for slot in range(5):
                    node = m - 3 + slot
                    if node >= 0:
                        term = float(table[m, slot]) * d_hist[l - 1][node]
                        quad = term if quad is None else quad + term
                total = total + (quad + g_now[l - 1] - e_hist[l - 1][m])
            rhs.append(total)
        solved = column_solve(jnp.stack(rhs, 0), inverse)
        for i, l in enumerate(moving):
            states[l] = solved[i]
    result = jnp.stack(states, 0)
    out = jnp.zeros((1,) + own_fields.shape[:1] + fields.shape[1:], jnp.float32)
    out = lax.dynamic_update_slice_in_dim(
        out, lax.dynamic_index_in_dim(result, me, 0), start, 2
    )
    for shift in range(1, depth):
        pairs = [(c, (c + shift) % depth) for c in range(depth)]
        sent = lax.dynamic_index_in_dim(result, (me + shift) % depth, 0)
        half = sent.shape[3] // 2
        got = jnp.concatenate(
            [
                lax.ppermute(sent[:, :, :, :half], "corr", pairs),
                lax.ppermute(sent[:, :, :, half:], "corr", pairs),
            ],
            3,
        )
        origin = (me - shift) % depth
        out = lax.dynamic_update_slice_in_dim(
            out, got, slab_of(origin, tile, depth) * slab, 2
        )
    return out


def solution(mesh):
    placed = (P(None, "tx", "ty", None), P(None, "tx", "ty", None), P())
    return jax.shard_map(
        on_device,
        mesh=mesh,
        in_specs=placed,
        out_specs=P("corr", None, "tx", "ty", None),
        check_vma=False,
    )
```

```python
import jax
import jax.numpy as jnp
import numpy as np
from jax import lax
from jax.experimental import pallas as pl
from jax.experimental.pallas import tpu as pltpu
from jax.sharding import PartitionSpec as P

STEPS = 8


DT = 0.1
A_RATE = 1.0
B_RATE = 3.0


def quad_cycle(count):
    table = np.zeros((count, 5))
    for m in range(count):
        first = max(0, m - 3)
        nodes = [float(j - m) for j in range(first, m + 2)]
        for i, xi in enumerate(nodes):
            coeffs = [1.0]
            for xo in nodes:
                if xo != xi:
                    widened = [0.0] * (len(coeffs) + 1)
                    for k, c in enumerate(coeffs):
                        widened[k] = widened[k] - xo * c / (xi - xo)
                        widened[k + 1] = widened[k + 1] + c / (xi - xo)
                    coeffs = widened
            integral = 0.0
            for k, c in enumerate(coeffs):
                integral = integral + c / (k + 1)
            table[m, first + i - (m - 3)] = integral
    return table


def thomas_kernel(up_ref, low_ref, out_ref, c_ref, d_ref):
    n = out_ref.shape[0]
    shape = out_ref.shape[1:]
    lanes = lax.broadcasted_iota(jnp.int32, shape, 1)
    species = lax.broadcasted_iota(jnp.int32, shape, 0)
    zero = jnp.zeros(shape, jnp.float32)

    def column(ref, j):
        value = jnp.full(shape, ref[0, j], jnp.float32)
        for s in range(1, shape[0]):
            value = jnp.where(species == s, ref[s, j], value)
        return value

    def forward(j, carry):
        cprev, dprev = carry
        up = column(up_ref, j)
        low = column(low_ref, j)
        inv = 1.0 / ((1.0 + low + up) + low * cprev)
        c = -up * inv
        d = (jnp.where(lanes == j, 1.0, 0.0) + low * dprev) * inv
        c_ref[j] = c
        d_ref[j] = d
        return c, d

    lax.fori_loop(0, n, forward, (zero, zero))

    def backward(i, x):
        j = n - 1 - i
        x = d_ref[j] - c_ref[j] * x
        out_ref[j] = x
        return x

    lax.fori_loop(0, n, backward, zero)


def vertical(diffusion):
    species, depth = diffusion.shape
    keep = (jnp.arange(depth) < depth - 1).astype(jnp.float32)
    upper = diffusion * keep[None, :]
    lower = jnp.concatenate([jnp.zeros((species, 1), jnp.float32), upper[:, :-1]], 1)
    rows = pl.pallas_call(
        thomas_kernel,
        out_shape=jax.ShapeDtypeStruct((depth, species, depth), jnp.float32),
        in_specs=[pl.BlockSpec(memory_space=pltpu.SMEM)] * 2,
        scratch_shapes=[pltpu.VMEM((depth, species, depth), jnp.float32)] * 2,
        cost_estimate=pl.CostEstimate(
            flops=12 * depth * species * depth,
            transcendentals=0,
            bytes_accessed=4 * 2 * depth * species * depth,
        ),
    )(upper, lower)
    inverse = jnp.transpose(rows, (1, 0, 2))
    return (inverse, upper, lower)


def vertical_apply(w, upper, lower):
    zero_col = jnp.zeros(w.shape[:-1] + (1,), jnp.float32)
    beneath = jnp.concatenate([zero_col, w[..., :-1]], -1)
    overhead = jnp.concatenate([w[..., 1:], zero_col], -1)
    lo = lower[:, None, None, :]
    up = upper[:, None, None, :]
    return (lo + up) * w - lo * beneath - up * overhead


def slab_of(corr, tile, depth):
    return jnp.where(tile % 2 == 0, corr, depth - 1 - corr)


def x_ring():
    depth, tiles = lax.axis_size("corr"), lax.axis_size("tx")
    order = []
    for tile in range(tiles):
        for q in range(depth):
            corr = q if tile % 2 == 0 else depth - 1 - q
            order.append(corr * tiles + tile)
    return order


def ring_halo(block, axes, order, dim, width):
    size = len(order)
    length = block.shape[dim]
    up = [(order[g], order[(g + 1) % size]) for g in range(size)]
    down = [(j, i) for i, j in up]
    last = lax.slice_in_dim(block, length - width, length, axis=dim)
    first = lax.slice_in_dim(block, 0, width, axis=dim)
    if size == 2:
        got = lax.ppermute(jnp.concatenate([first, last], dim), axes, up)
        after = lax.slice_in_dim(got, 0, width, axis=dim)
        before = lax.slice_in_dim(got, width, 2 * width, axis=dim)
        return before, after
    before = lax.ppermute(last, axes, up)
    after = lax.ppermute(first, axes, down)
    return before, after


def tendency(state, wind):
    west, east = ring_halo(state, ("corr", "tx"), x_ring(), 2, 2)
    south, north = ring_halo(state, ("ty",), list(range(lax.axis_size("ty"))), 3, 2)
    px = jnp.concatenate([west, state, east], 2)
    py = jnp.concatenate([south, state, north], 3)
    center = state
    twelfth = 1.0 / 12.0
    far_x = px[:, :, :-4] - px[:, :, 4:]
    near_x = px[:, :, 3:-1] - px[:, :, 1:-3]
    far_sum_x = px[:, :, :-4] + px[:, :, 4:]
    near_sum_x = px[:, :, 3:-1] + px[:, :, 1:-3]
    far_y = py[:, :, :, :-4] - py[:, :, :, 4:]
    near_y = py[:, :, :, 3:-1] - py[:, :, :, 1:-3]
    far_sum_y = py[:, :, :, :-4] + py[:, :, :, 4:]
    near_sum_y = py[:, :, :, 3:-1] + py[:, :, :, 1:-3]
    dx1 = (far_x + 8.0 * near_x) * twelfth
    dy1 = (far_y + 8.0 * near_y) * twelfth
    laplace = (
        16.0 * (near_sum_x + near_sum_y) - (far_sum_x + far_sum_y) - 60.0 * center
    ) * twelfth
    kappa = jnp.array([0.5, 1.0], jnp.float32)[None, :, None, None, None]
    first = center[:, 0]
    second = center[:, 1]
    square_term = first * first * second
    react = jnp.stack(
        [A_RATE - (B_RATE + 1.0) * first + square_term, B_RATE * first - square_term], 1
    )
    flow = -(wind[0][None, None] * dx1 + wind[1][None, None] * dy1)
    return DT * (flow + kappa * laplace + react)


def column_solve(rhs, inverse):
    return jnp.einsum(
        "lsxyk,sjk->lsxyj", rhs, inverse, precision=lax.Precision.HIGHEST
    )


def on_device(fields, wind, diffusion):
    inverse, upper, lower = vertical(diffusion)
    table = quad_cycle(STEPS)
    depth = lax.axis_size("corr")
    slab = fields.shape[1] // depth
    me = lax.axis_index("corr")
    tile = lax.axis_index("tx")
    start = slab_of(me, tile, depth) * slab
    own_fields = lax.dynamic_slice_in_dim(fields, start, slab, 1)
    own_wind = lax.dynamic_slice_in_dim(wind, start, slab, 1)

    states = [own_fields] * depth
    e_hist = [dict() for _ in range(depth)]
    d_hist = [dict() for _ in range(depth)]
    g_now = [None] * depth
    for k in range(STEPS + depth - 1):
        active = [
            l for l in range(depth)
            if 0 <= k - l < STEPS or (k - l == STEPS and l < depth - 1)
        ]
        stacked = jnp.stack([states[l] for l in active], 0)
        own_e = tendency(stacked, own_wind)
        feeds = [l for l in active if l < depth - 1]
        if feeds:
            lows = [active.index(l) for l in feeds]
            lo, hi = lows[0], lows[-1] + 1
            own_g = vertical_apply(stacked[lo:hi], upper, lower)
            for i, l in enumerate(feeds):
                m = k - l
                g_now[l] = own_g[i]
                d_hist[l][m] = own_e[lo + i] - own_g[i]
        moving = [l for l in active if k - l < STEPS]
        rhs = []
        for l in moving:
            m = k - l
            i = active.index(l)
            e_hist[l][m] = own_e[i]
            total = states[l] + own_e[i]
            if l > 0:
                quad = None
                for slot in range(5):
                    node = m - 3 + slot
                    if node >= 0:
                        term = float(table[m, slot]) * d_hist[l - 1][node]
                        quad = term if quad is None else quad + term
                total = total + (quad + g_now[l - 1] - e_hist[l - 1][m])
            rhs.append(total)
        solved = column_solve(jnp.stack(rhs, 0), inverse)
        for i, l in enumerate(moving):
            states[l] = solved[i]
    result = jnp.stack(states, 0)
    out = jnp.zeros((1,) + own_fields.shape[:1] + fields.shape[1:], jnp.float32)
    out = lax.dynamic_update_slice_in_dim(
        out, lax.dynamic_index_in_dim(result, me, 0), start, 2
    )
    for shift in range(1, depth):
        pairs = [(c, (c + shift) % depth) for c in range(depth)]
        sent = lax.dynamic_index_in_dim(result, (me + shift) % depth, 0)
        half = sent.shape[3] // 2
        got = jnp.concatenate(
            [
                lax.ppermute(sent[:, :, :, :half], "corr", pairs),
                lax.ppermute(sent[:, :, :, half:], "corr", pairs),
            ],
            3,
        )
        origin = (me - shift) % depth
        out = lax.dynamic_update_slice_in_dim(
            out, got, slab_of(origin, tile, depth) * slab, 2
        )
    return out


def solution(mesh):
    placed = (P(None, "tx", "ty", None), P(None, "tx", "ty", None), P())
    return jax.shard_map(
        on_device,
        mesh=mesh,
        in_specs=placed,
        out_specs=P("corr", None, "tx", "ty", None),
        check_vma=False,
    )
```

```python
import jax
import jax.numpy as jnp
import numpy as np
from jax import lax
from jax.experimental import pallas as pl
from jax.experimental.pallas import tpu as pltpu
from jax.sharding import PartitionSpec as P

STEPS = 8


DT = 0.1
A_RATE = 1.0
B_RATE = 3.0


def quad_cycle(count):
    table = np.zeros((count, 5))
    for m in range(count):
        first = max(0, m - 3)
        nodes = [float(j - m) for j in range(first, m + 2)]
        for i, xi in enumerate(nodes):
            coeffs = [1.0]
            for xo in nodes:
                if xo != xi:
                    widened = [0.0] * (len(coeffs) + 1)
                    for k, c in enumerate(coeffs):
                        widened[k] = widened[k] - xo * c / (xi - xo)
                        widened[k + 1] = widened[k + 1] + c / (xi - xo)
                    coeffs = widened
            integral = 0.0
            for k, c in enumerate(coeffs):
                integral = integral + c / (k + 1)
            table[m, first + i - (m - 3)] = integral
    return table


def thomas_kernel(up_ref, low_ref, out_ref, c_ref, d_ref):
    n = out_ref.shape[0]
    shape = out_ref.shape[1:]
    lanes = lax.broadcasted_iota(jnp.int32, shape, 1)
    species = lax.broadcasted_iota(jnp.int32, shape, 0)
    zero = jnp.zeros(shape, jnp.float32)

    def column(ref, j):
        value = jnp.full(shape, ref[0, j], jnp.float32)
        for s in range(1, shape[0]):
            value = jnp.where(species == s, ref[s, j], value)
        return value

    def forward(j, carry):
        cprev, dprev = carry
        up = column(up_ref, j)
        low = column(low_ref, j)
        inv = 1.0 / ((1.0 + low + up) + low * cprev)
        c = -up * inv
        d = (jnp.where(lanes == j, 1.0, 0.0) + low * dprev) * inv
        c_ref[j] = c
        d_ref[j] = d
        return c, d

    lax.fori_loop(0, n, forward, (zero, zero))

    def backward(i, x):
        j = n - 1 - i
        x = d_ref[j] - c_ref[j] * x
        out_ref[j] = x
        return x

    lax.fori_loop(0, n, backward, zero)


def vertical(diffusion):
    species, depth = diffusion.shape
    keep = (jnp.arange(depth) < depth - 1).astype(jnp.float32)
    upper = diffusion * keep[None, :]
    lower = jnp.concatenate([jnp.zeros((species, 1), jnp.float32), upper[:, :-1]], 1)
    rows = pl.pallas_call(
        thomas_kernel,
        out_shape=jax.ShapeDtypeStruct((depth, species, depth), jnp.float32),
        in_specs=[pl.BlockSpec(memory_space=pltpu.SMEM)] * 2,
        scratch_shapes=[pltpu.VMEM((depth, species, depth), jnp.float32)] * 2,
        cost_estimate=pl.CostEstimate(
            flops=12 * depth * species * depth,
            transcendentals=0,
            bytes_accessed=4 * 2 * depth * species * depth,
        ),
    )(upper, lower)
    inverse = jnp.transpose(rows, (1, 0, 2))
    return (inverse, upper, lower)


def vertical_apply(w, upper, lower):
    zero_col = jnp.zeros(w.shape[:-1] + (1,), jnp.float32)
    beneath = jnp.concatenate([zero_col, w[..., :-1]], -1)
    overhead = jnp.concatenate([w[..., 1:], zero_col], -1)
    lo = lower[:, None, None, :]
    up = upper[:, None, None, :]
    return (lo + up) * w - lo * beneath - up * overhead


def slab_of(corr, tile, depth):
    return jnp.where(tile % 2 == 0, corr, depth - 1 - corr)


def x_ring():
    depth, tiles = lax.axis_size("corr"), lax.axis_size("tx")
    order = []
    for tile in range(tiles):
        for q in range(depth):
            corr = q if tile % 2 == 0 else depth - 1 - q
            order.append(corr * tiles + tile)
    return order


def ring_halo(block, axes, order, dim, width):
    size = len(order)
    length = block.shape[dim]
    up = [(order[g], order[(g + 1) % size]) for g in range(size)]
    down = [(j, i) for i, j in up]
    last = lax.slice_in_dim(block, length - width, length, axis=dim)
    first = lax.slice_in_dim(block, 0, width, axis=dim)
    if size == 2:
        got = lax.ppermute(jnp.concatenate([first, last], dim), axes, up)
        after = lax.slice_in_dim(got, 0, width, axis=dim)
        before = lax.slice_in_dim(got, width, 2 * width, axis=dim)
        return before, after
    before = lax.ppermute(last, axes, up)
    after = lax.ppermute(first, axes, down)
    return before, after


def tendency(state, wind):
    west, east = ring_halo(state, ("corr", "tx"), x_ring(), 2, 2)
    south, north = ring_halo(state, ("ty",), list(range(lax.axis_size("ty"))), 3, 2)
    px = jnp.concatenate([west, state, east], 2)
    py = jnp.concatenate([south, state, north], 3)
    center = state
    twelfth = 1.0 / 12.0
    far_x = px[:, :, :-4] - px[:, :, 4:]
    near_x = px[:, :, 3:-1] - px[:, :, 1:-3]
    far_sum_x = px[:, :, :-4] + px[:, :, 4:]
    near_sum_x = px[:, :, 3:-1] + px[:, :, 1:-3]
    far_y = py[:, :, :, :-4] - py[:, :, :, 4:]
    near_y = py[:, :, :, 3:-1] - py[:, :, :, 1:-3]
    far_sum_y = py[:, :, :, :-4] + py[:, :, :, 4:]
    near_sum_y = py[:, :, :, 3:-1] + py[:, :, :, 1:-3]
    dx1 = (far_x + 8.0 * near_x) * twelfth
    dy1 = (far_y + 8.0 * near_y) * twelfth
    laplace = (
        16.0 * (near_sum_x + near_sum_y) - (far_sum_x + far_sum_y) - 60.0 * center
    ) * twelfth
    kappa = jnp.array([0.5, 1.0], jnp.float32)[None, :, None, None, None]
    first = center[:, 0]
    second = center[:, 1]
    square_term = first * first * second
    react = jnp.stack(
        [A_RATE - (B_RATE + 1.0) * first + square_term, B_RATE * first - square_term], 1
    )
    flow = -(wind[0][None, None] * dx1 + wind[1][None, None] * dy1)
    return DT * (flow + kappa * laplace + react)


def column_solve(rhs, inverse):
    return jnp.einsum(
        "lsxyk,sjk->lsxyj", rhs, inverse, precision=lax.Precision.HIGH
    )


def on_device(fields, wind, diffusion):
    inverse, upper, lower = vertical(diffusion)
    table = quad_cycle(STEPS)
    depth = lax.axis_size("corr")
    slab = fields.shape[1] // depth
    me = lax.axis_index("corr")
    tile = lax.axis_index("tx")
    start = slab_of(me, tile, depth) * slab
    own_fields = lax.dynamic_slice_in_dim(fields, start, slab, 1)
    own_wind = lax.dynamic_slice_in_dim(wind, start, slab, 1)

    states = [own_fields] * depth
    e_hist = [dict() for _ in range(depth)]
    d_hist = [dict() for _ in range(depth)]
    g_now = [None] * depth
    for k in range(STEPS + depth - 1):
        active = [
            l for l in range(depth)
            if 0 <= k - l < STEPS or (k - l == STEPS and l < depth - 1)
        ]
        stacked = jnp.stack([states[l] for l in active], 0)
        own_e = tendency(stacked, own_wind)
        feeds = [l for l in active if l < depth - 1]
        if feeds:
            lows = [active.index(l) for l in feeds]
            lo, hi = lows[0], lows[-1] + 1
            own_g = vertical_apply(stacked[lo:hi], upper, lower)
            for i, l in enumerate(feeds):
                m = k - l
                g_now[l] = own_g[i]
                d_hist[l][m] = own_e[lo + i] - own_g[i]
        moving = [l for l in active if k - l < STEPS]
        rhs = []
        for l in moving:
            m = k - l
            i = active.index(l)
            e_hist[l][m] = own_e[i]
            total = states[l] + own_e[i]
            if l > 0:
                quad = None
                for slot in range(5):
                    node = m - 3 + slot
                    if node >= 0:
                        term = float(table[m, slot]) * d_hist[l - 1][node]
                        quad = term if quad is None else quad + term
                total = total + (quad + g_now[l - 1] - e_hist[l - 1][m])
            rhs.append(total)
        solved = column_solve(jnp.stack(rhs, 0), inverse)
        for i, l in enumerate(moving):
            states[l] = solved[i]
    result = jnp.stack(states, 0)
    out = jnp.zeros((1,) + own_fields.shape[:1] + fields.shape[1:], jnp.float32)
    out = lax.dynamic_update_slice_in_dim(
        out, lax.dynamic_index_in_dim(result, me, 0), start, 2
    )
    for shift in range(1, depth):
        pairs = [(c, (c + shift) % depth) for c in range(depth)]
        sent = lax.dynamic_index_in_dim(result, (me + shift) % depth, 0)
        half = sent.shape[3] // 2
        got = jnp.concatenate(
            [
                lax.ppermute(sent[:, :, :, :half], "corr", pairs),
                lax.ppermute(sent[:, :, :, half:], "corr", pairs),
            ],
            3,
        )
        origin = (me - shift) % depth
        out = lax.dynamic_update_slice_in_dim(
            out, got, slab_of(origin, tile, depth) * slab, 2
        )
    return out


def solution(mesh):
    placed = (P(None, "tx", "ty", None), P(None, "tx", "ty", None), P())
    return jax.shard_map(
        on_device,
        mesh=mesh,
        in_specs=placed,
        out_specs=P("corr", None, "tx", "ty", None),
        check_vma=False,
    )
```

```python
import jax
import jax.numpy as jnp
import numpy as np
from jax import lax
from jax.experimental import pallas as pl
from jax.experimental.pallas import tpu as pltpu
from jax.sharding import PartitionSpec as P

STEPS = 8


DT = 0.1
A_RATE = 1.0
B_RATE = 3.0


def quad_cycle(count):
    table = np.zeros((count, 5))
    for m in range(count):
        first = max(0, m - 3)
        nodes = [float(j - m) for j in range(first, m + 2)]
        for i, xi in enumerate(nodes):
            coeffs = [1.0]
            for xo in nodes:
                if xo != xi:
                    widened = [0.0] * (len(coeffs) + 1)
                    for k, c in enumerate(coeffs):
                        widened[k] = widened[k] - xo * c / (xi - xo)
                        widened[k + 1] = widened[k + 1] + c / (xi - xo)
                    coeffs = widened
            integral = 0.0
            for k, c in enumerate(coeffs):
                integral = integral + c / (k + 1)
            table[m, first + i - (m - 3)] = integral
    return table


def thomas_kernel(up_ref, low_ref, out_ref, c_ref, d_ref):
    n = out_ref.shape[0]
    shape = out_ref.shape[1:]
    lanes = lax.broadcasted_iota(jnp.int32, shape, 1)
    species = lax.broadcasted_iota(jnp.int32, shape, 0)
    zero = jnp.zeros(shape, jnp.float32)

    def column(ref, j):
        value = jnp.full(shape, ref[0, j], jnp.float32)
        for s in range(1, shape[0]):
            value = jnp.where(species == s, ref[s, j], value)
        return value

    def forward(j, carry):
        cprev, dprev = carry
        up = column(up_ref, j)
        low = column(low_ref, j)
        inv = 1.0 / ((1.0 + low + up) + low * cprev)
        c = -up * inv
        d = (jnp.where(lanes == j, 1.0, 0.0) + low * dprev) * inv
        c_ref[j] = c
        d_ref[j] = d
        return c, d

    lax.fori_loop(0, n, forward, (zero, zero))

    def backward(i, x):
        j = n - 1 - i
        x = d_ref[j] - c_ref[j] * x
        out_ref[j] = x
        return x

    lax.fori_loop(0, n, backward, zero)


def vertical(diffusion):
    species, depth = diffusion.shape
    keep = (jnp.arange(depth) < depth - 1).astype(jnp.float32)
    upper = diffusion * keep[None, :]
    lower = jnp.concatenate([jnp.zeros((species, 1), jnp.float32), upper[:, :-1]], 1)
    rows = pl.pallas_call(
        thomas_kernel,
        out_shape=jax.ShapeDtypeStruct((depth, species, depth), jnp.float32),
        in_specs=[pl.BlockSpec(memory_space=pltpu.SMEM)] * 2,
        scratch_shapes=[pltpu.VMEM((depth, species, depth), jnp.float32)] * 2,
        cost_estimate=pl.CostEstimate(
            flops=12 * depth * species * depth,
            transcendentals=0,
            bytes_accessed=4 * 2 * depth * species * depth,
        ),
    )(upper, lower)
    inverse = jnp.transpose(rows, (1, 0, 2))
    return (inverse, upper, lower)


def vertical_apply(w, upper, lower):
    zero_col = jnp.zeros(w.shape[:-1] + (1,), jnp.float32)
    beneath = jnp.concatenate([zero_col, w[..., :-1]], -1)
    overhead = jnp.concatenate([w[..., 1:], zero_col], -1)
    lo = lower[:, None, None, :]
    up = upper[:, None, None, :]
    return (lo + up) * w - lo * beneath - up * overhead


def slab_of(corr, tile, depth):
    return jnp.where(tile % 2 == 0, corr, depth - 1 - corr)


def x_ring():
    depth, tiles = lax.axis_size("corr"), lax.axis_size("tx")
    order = []
    for tile in range(tiles):
        for q in range(depth):
            corr = q if tile % 2 == 0 else depth - 1 - q
            order.append(corr * tiles + tile)
    return order


def ring_halo(block, axes, order, dim, width):
    size = len(order)
    length = block.shape[dim]
    up = [(order[g], order[(g + 1) % size]) for g in range(size)]
    down = [(j, i) for i, j in up]
    last = lax.slice_in_dim(block, length - width, length, axis=dim)
    first = lax.slice_in_dim(block, 0, width, axis=dim)
    if size == 2:
        got = lax.ppermute(jnp.concatenate([first, last], dim), axes, up)
        after = lax.slice_in_dim(got, 0, width, axis=dim)
        before = lax.slice_in_dim(got, width, 2 * width, axis=dim)
        return before, after
    before = lax.ppermute(last, axes, up)
    after = lax.ppermute(first, axes, down)
    return before, after


def tendency(state, wind):
    west, east = ring_halo(state, ("corr", "tx"), x_ring(), 2, 2)
    south, north = ring_halo(state, ("ty",), list(range(lax.axis_size("ty"))), 3, 2)
    px = jnp.concatenate([west, state, east], 2)
    py = jnp.concatenate([south, state, north], 3)
    center = state
    twelfth = 1.0 / 12.0
    far_x = px[:, :, :-4] - px[:, :, 4:]
    near_x = px[:, :, 3:-1] - px[:, :, 1:-3]
    far_sum_x = px[:, :, :-4] + px[:, :, 4:]
    near_sum_x = px[:, :, 3:-1] + px[:, :, 1:-3]
    far_y = py[:, :, :, :-4] - py[:, :, :, 4:]
    near_y = py[:, :, :, 3:-1] - py[:, :, :, 1:-3]
    far_sum_y = py[:, :, :, :-4] + py[:, :, :, 4:]
    near_sum_y = py[:, :, :, 3:-1] + py[:, :, :, 1:-3]
    dx1 = (far_x + 8.0 * near_x) * twelfth
    dy1 = (far_y + 8.0 * near_y) * twelfth
    laplace = (
        16.0 * (near_sum_x + near_sum_y) - (far_sum_x + far_sum_y) - 60.0 * center
    ) * twelfth
    kappa = jnp.array([0.5, 1.0], jnp.float32)[None, :, None, None, None]
    first = center[:, 0]
    second = center[:, 1]
    square_term = first * first * second
    react = jnp.stack(
        [A_RATE - (B_RATE + 1.0) * first + square_term, B_RATE * first - square_term], 1
    )
    flow = -(wind[0][None, None] * dx1 + wind[1][None, None] * dy1)
    return DT * (flow + kappa * laplace + react)


def column_solve(rhs, inverse):
    return jnp.einsum(
        "lsxyk,sjk->lsxyj", rhs, inverse, precision=lax.Precision.HIGHEST
    )


def on_device(fields, wind, diffusion):
    inverse, upper, lower = vertical(diffusion)
    table = quad_cycle(STEPS)
    depth = lax.axis_size("corr")
    slab = fields.shape[1] // depth
    me = lax.axis_index("corr")
    tile = lax.axis_index("tx")
    start = slab_of(me, tile, depth) * slab
    own_fields = lax.dynamic_slice_in_dim(fields, start, slab, 1)
    own_wind = lax.dynamic_slice_in_dim(wind, start, slab, 1)

    states = [own_fields] * depth
    e_hist = [dict() for _ in range(depth)]
    d_hist = [dict() for _ in range(depth)]
    g_now = [None] * depth
    for k in range(STEPS + depth - 1):
        active = [
            l for l in range(depth)
            if 0 <= k - l < STEPS or (k - l == STEPS and l < depth - 1)
        ]
        stacked = jnp.stack([states[l] for l in active], 0)
        own_e = tendency(stacked, own_wind)
        feeds = [l for l in active if l < depth - 1]
        if feeds:
            lows = [active.index(l) for l in feeds]
            lo, hi = lows[0], lows[-1] + 1
            own_g = vertical_apply(stacked[lo:hi], upper, lower)
            for i, l in enumerate(feeds):
                m = k - l
                g_now[l] = own_g[i]
                d_hist[l][m] = own_e[lo + i] - own_g[i]
        moving = [l for l in active if k - l < STEPS]
        known, fresh = [], []
        for l in moving:
            m = k - l
            i = active.index(l)
            e_hist[l][m] = own_e[i]
            before = states[l]
            after = own_e[i]
            if l > 0:
                last = float(table[m, 4])
                quad = None
                for slot in range(4):
                    node = m - 3 + slot
                    if node >= 0:
                        term = float(table[m, slot]) * d_hist[l - 1][node]
                        quad = term if quad is None else quad + term
                older = (1.0 - last) * g_now[l - 1] - e_hist[l - 1][m]
                before = before + (older if quad is None else quad + older)
                after = after + last * own_e[active.index(l - 1)]
            known.append(before)
            fresh.append(after)
        solved = column_solve(jnp.stack(known, 0), inverse) + column_solve(
            jnp.stack(fresh, 0), inverse
        )
        for i, l in enumerate(moving):
            states[l] = solved[i]
    result = jnp.stack(states, 0)
    out = jnp.zeros((1,) + own_fields.shape[:1] + fields.shape[1:], jnp.float32)
    out = lax.dynamic_update_slice_in_dim(
        out, lax.dynamic_index_in_dim(result, me, 0), start, 2
    )
    for shift in range(1, depth):
        pairs = [(c, (c + shift) % depth) for c in range(depth)]
        sent = lax.dynamic_index_in_dim(result, (me + shift) % depth, 0)
        half = sent.shape[3] // 2
        got = jnp.concatenate(
            [
                lax.ppermute(sent[:, :, :, :half], "corr", pairs),
                lax.ppermute(sent[:, :, :, half:], "corr", pairs),
            ],
            3,
        )
        origin = (me - shift) % depth
        out = lax.dynamic_update_slice_in_dim(
            out, got, slab_of(origin, tile, depth) * slab, 2
        )
    return out


def solution(mesh):
    placed = (P(None, "tx", "ty", None), P(None, "tx", "ty", None), P())
    return jax.shard_map(
        on_device,
        mesh=mesh,
        in_specs=placed,
        out_specs=P("corr", None, "tx", "ty", None),
        check_vma=False,
    )
```

```python
import jax
import jax.numpy as jnp
import numpy as np
from jax import lax
from jax.experimental import pallas as pl
from jax.experimental.pallas import tpu as pltpu
from jax.sharding import PartitionSpec as P

STEPS = 8


DT = 0.1
A_RATE = 1.0
B_RATE = 3.0


def quad_cycle(count):
    table = np.zeros((count, 5))
    for m in range(count):
        first = max(0, m - 3)
        nodes = [float(j - m) for j in range(first, m + 2)]
        for i, xi in enumerate(nodes):
            coeffs = [1.0]
            for xo in nodes:
                if xo != xi:
                    widened = [0.0] * (len(coeffs) + 1)
                    for k, c in enumerate(coeffs):
                        widened[k] = widened[k] - xo * c / (xi - xo)
                        widened[k + 1] = widened[k + 1] + c / (xi - xo)
                    coeffs = widened
            integral = 0.0
            for k, c in enumerate(coeffs):
                integral = integral + c / (k + 1)
            table[m, first + i - (m - 3)] = integral
    return table


def thomas_kernel(up_ref, low_ref, out_ref, c_ref, d_ref):
    n = out_ref.shape[0]
    shape = out_ref.shape[1:]
    lanes = lax.broadcasted_iota(jnp.int32, shape, 1)
    species = lax.broadcasted_iota(jnp.int32, shape, 0)
    zero = jnp.zeros(shape, jnp.float32)

    def column(ref, j):
        value = jnp.full(shape, ref[0, j], jnp.float32)
        for s in range(1, shape[0]):
            value = jnp.where(species == s, ref[s, j], value)
        return value

    def forward(j, carry):
        cprev, dprev = carry
        up = column(up_ref, j)
        low = column(low_ref, j)
        inv = 1.0 / ((1.0 + low + up) + low * cprev)
        c = -up * inv
        d = (jnp.where(lanes == j, 1.0, 0.0) + low * dprev) * inv
        c_ref[j] = c
        d_ref[j] = d
        return c, d

    lax.fori_loop(0, n, forward, (zero, zero), unroll=8)

    def backward(i, x):
        j = n - 1 - i
        x = d_ref[j] - c_ref[j] * x
        out_ref[j] = x
        return x

    lax.fori_loop(0, n, backward, zero, unroll=8)


def vertical(diffusion):
    species, depth = diffusion.shape
    keep = (jnp.arange(depth) < depth - 1).astype(jnp.float32)
    upper = diffusion * keep[None, :]
    lower = jnp.concatenate([jnp.zeros((species, 1), jnp.float32), upper[:, :-1]], 1)
    rows = pl.pallas_call(
        thomas_kernel,
        out_shape=jax.ShapeDtypeStruct((depth, species, depth), jnp.float32),
        in_specs=[pl.BlockSpec(memory_space=pltpu.SMEM)] * 2,
        scratch_shapes=[pltpu.VMEM((depth, species, depth), jnp.float32)] * 2,
        cost_estimate=pl.CostEstimate(
            flops=12 * depth * species * depth,
            transcendentals=0,
            bytes_accessed=4 * 2 * depth * species * depth,
        ),
    )(upper, lower)
    inverse = jnp.transpose(rows, (1, 0, 2))
    return (inverse, upper, lower)


def vertical_apply(w, upper, lower):
    zero_col = jnp.zeros(w.shape[:-1] + (1,), jnp.float32)
    beneath = jnp.concatenate([zero_col, w[..., :-1]], -1)
    overhead = jnp.concatenate([w[..., 1:], zero_col], -1)
    lo = lower[:, None, None, :]
    up = upper[:, None, None, :]
    return (lo + up) * w - lo * beneath - up * overhead


def slab_of(corr, tile, depth):
    return jnp.where(tile % 2 == 0, corr, depth - 1 - corr)


def x_ring():
    depth, tiles = lax.axis_size("corr"), lax.axis_size("tx")
    order = []
    for tile in range(tiles):
        for q in range(depth):
            corr = q if tile % 2 == 0 else depth - 1 - q
            order.append(corr * tiles + tile)
    return order


def ring_halo(block, axes, order, dim, width):
    size = len(order)
    length = block.shape[dim]
    up = [(order[g], order[(g + 1) % size]) for g in range(size)]
    down = [(j, i) for i, j in up]
    last = lax.slice_in_dim(block, length - width, length, axis=dim)
    first = lax.slice_in_dim(block, 0, width, axis=dim)
    if size == 2:
        got = lax.ppermute(jnp.concatenate([first, last], dim), axes, up)
        after = lax.slice_in_dim(got, 0, width, axis=dim)
        before = lax.slice_in_dim(got, width, 2 * width, axis=dim)
        return before, after
    before = lax.ppermute(last, axes, up)
    after = lax.ppermute(first, axes, down)
    return before, after


def tendency(state, wind):
    west, east = ring_halo(state, ("corr", "tx"), x_ring(), 2, 2)
    south, north = ring_halo(state, ("ty",), list(range(lax.axis_size("ty"))), 3, 2)
    px = jnp.concatenate([west, state, east], 2)
    py = jnp.concatenate([south, state, north], 3)
    center = state
    twelfth = 1.0 / 12.0
    far_x = px[:, :, :-4] - px[:, :, 4:]
    near_x = px[:, :, 3:-1] - px[:, :, 1:-3]
    far_sum_x = px[:, :, :-4] + px[:, :, 4:]
    near_sum_x = px[:, :, 3:-1] + px[:, :, 1:-3]
    far_y = py[:, :, :, :-4] - py[:, :, :, 4:]
    near_y = py[:, :, :, 3:-1] - py[:, :, :, 1:-3]
    far_sum_y = py[:, :, :, :-4] + py[:, :, :, 4:]
    near_sum_y = py[:, :, :, 3:-1] + py[:, :, :, 1:-3]
    dx1 = (far_x + 8.0 * near_x) * twelfth
    dy1 = (far_y + 8.0 * near_y) * twelfth
    laplace = (
        16.0 * (near_sum_x + near_sum_y) - (far_sum_x + far_sum_y) - 60.0 * center
    ) * twelfth
    kappa = jnp.array([0.5, 1.0], jnp.float32)[None, :, None, None, None]
    first = center[:, 0]
    second = center[:, 1]
    square_term = first * first * second
    react = jnp.stack(
        [A_RATE - (B_RATE + 1.0) * first + square_term, B_RATE * first - square_term], 1
    )
    flow = -(wind[0][None, None] * dx1 + wind[1][None, None] * dy1)
    return DT * (flow + kappa * laplace + react)


def column_solve(rhs, inverse):
    return jnp.einsum(
        "lsxyk,sjk->lsxyj", rhs, inverse, precision=lax.Precision.HIGHEST
    )


def on_device(fields, wind, diffusion):
    inverse, upper, lower = vertical(diffusion)
    table = quad_cycle(STEPS)
    depth = lax.axis_size("corr")
    slab = fields.shape[1] // depth
    me = lax.axis_index("corr")
    tile = lax.axis_index("tx")
    start = slab_of(me, tile, depth) * slab
    own_fields = lax.dynamic_slice_in_dim(fields, start, slab, 1)
    own_wind = lax.dynamic_slice_in_dim(wind, start, slab, 1)

    states = [own_fields] * depth
    e_hist = [dict() for _ in range(depth)]
    d_hist = [dict() for _ in range(depth)]
    g_now = [None] * depth
    for k in range(STEPS + depth - 1):
        active = [
            l for l in range(depth)
            if 0 <= k - l < STEPS or (k - l == STEPS and l < depth - 1)
        ]
        stacked = jnp.stack([states[l] for l in active], 0)
        own_e = tendency(stacked, own_wind)
        feeds = [l for l in active if l < depth - 1]
        if feeds:
            lows = [active.index(l) for l in feeds]
            lo, hi = lows[0], lows[-1] + 1
            own_g = vertical_apply(stacked[lo:hi], upper, lower)
            for i, l in enumerate(feeds):
                m = k - l
                g_now[l] = own_g[i]
                d_hist[l][m] = own_e[lo + i] - own_g[i]
        moving = [l for l in active if k - l < STEPS]
        rhs = []
        for l in moving:
            m = k - l
            i = active.index(l)
            e_hist[l][m] = own_e[i]
            total = states[l] + own_e[i]
            if l > 0:
                quad = None
                for slot in range(5):
                    node = m - 3 + slot
                    if node >= 0:
                        term = float(table[m, slot]) * d_hist[l - 1][node]
                        quad = term if quad is None else quad + term
                total = total + (quad + g_now[l - 1] - e_hist[l - 1][m])
            rhs.append(total)
        solved = column_solve(jnp.stack(rhs, 0), inverse)
        for i, l in enumerate(moving):
            states[l] = solved[i]
    out = jnp.zeros((1,) + own_fields.shape[:1] + fields.shape[1:], jnp.float32)
    out = lax.dynamic_update_slice_in_dim(
        out, jnp.stack(states, 0)[me][None], start, 2
    )
    for shift in range(1, depth):
        origin = (me - shift) % depth
        got = None
        for level in range(depth):
            pairs = [((level + shift) % depth, level)]
            arrived = lax.ppermute(states[level][None], "corr", pairs)
            got = arrived if got is None else jnp.where(me == level, arrived, got)
        out = lax.dynamic_update_slice_in_dim(
            out, got, slab_of(origin, tile, depth) * slab, 2
        )
    return out


def solution(mesh):
    placed = (P(None, "tx", "ty", None), P(None, "tx", "ty", None), P())
    return jax.shard_map(
        on_device,
        mesh=mesh,
        in_specs=placed,
        out_specs=P("corr", None, "tx", "ty", None),
        check_vma=False,
    )
```

```python
import jax
import jax.numpy as jnp
import numpy as np
from jax import lax
from jax.experimental import pallas as pl
from jax.experimental.pallas import tpu as pltpu
from jax.sharding import PartitionSpec as P

STEPS = 8


DT = 0.1
A_RATE = 1.0
B_RATE = 3.0


def quad_cycle(count):
    table = np.zeros((count, 5))
    for m in range(count):
        first = max(0, m - 3)
        nodes = [float(j - m) for j in range(first, m + 2)]
        for i, xi in enumerate(nodes):
            coeffs = [1.0]
            for xo in nodes:
                if xo != xi:
                    widened = [0.0] * (len(coeffs) + 1)
                    for k, c in enumerate(coeffs):
                        widened[k] = widened[k] - xo * c / (xi - xo)
                        widened[k + 1] = widened[k + 1] + c / (xi - xo)
                    coeffs = widened
            integral = 0.0
            for k, c in enumerate(coeffs):
                integral = integral + c / (k + 1)
            table[m, first + i - (m - 3)] = integral
    return table


def thomas_kernel(diff_ref, out_ref, c_ref, d_ref):
    n = out_ref.shape[0]
    shape = out_ref.shape[1:]
    lanes = lax.broadcasted_iota(jnp.int32, shape, 1)
    species = lax.broadcasted_iota(jnp.int32, shape, 0)
    zero = jnp.zeros(shape, jnp.float32)

    def column(j):
        value = jnp.full(shape, diff_ref[0, j], jnp.float32)
        for s in range(1, shape[0]):
            value = jnp.where(species == s, diff_ref[s, j], value)
        return value

    def forward(j, carry):
        cprev, dprev = carry
        up = jnp.where(j < n - 1, column(j), 0.0)
        low = jnp.where(j > 0, column(jnp.maximum(j - 1, 0)), 0.0)
        inv = 1.0 / ((1.0 + low + up) + low * cprev)
        c = -up * inv
        d = (jnp.where(lanes == j, 1.0, 0.0) + low * dprev) * inv
        c_ref[j] = c
        d_ref[j] = d
        return c, d

    lax.fori_loop(0, n, forward, (zero, zero), unroll=8)

    def backward(i, x):
        j = n - 1 - i
        x = d_ref[j] - c_ref[j] * x
        out_ref[j] = x
        return x

    lax.fori_loop(0, n, backward, zero, unroll=8)


def vertical(diffusion):
    species, depth = diffusion.shape
    keep = (jnp.arange(depth) < depth - 1).astype(jnp.float32)
    upper = diffusion * keep[None, :]
    lower = jnp.concatenate([jnp.zeros((species, 1), jnp.float32), upper[:, :-1]], 1)
    rows = pl.pallas_call(
        thomas_kernel,
        out_shape=jax.ShapeDtypeStruct((depth, species, depth), jnp.float32),
        in_specs=[pl.BlockSpec(memory_space=pltpu.SMEM)],
        scratch_shapes=[pltpu.VMEM((depth, species, depth), jnp.float32)] * 2,
        cost_estimate=pl.CostEstimate(
            flops=12 * depth * species * depth,
            transcendentals=0,
            bytes_accessed=4 * 2 * depth * species * depth,
        ),
    )(diffusion)
    inverse = jnp.transpose(rows, (1, 0, 2))
    return (inverse, upper, lower)


def vertical_apply(w, upper, lower):
    zero_col = jnp.zeros(w.shape[:-1] + (1,), jnp.float32)
    beneath = jnp.concatenate([zero_col, w[..., :-1]], -1)
    overhead = jnp.concatenate([w[..., 1:], zero_col], -1)
    lo = lower[:, None, None, :]
    up = upper[:, None, None, :]
    return (lo + up) * w - lo * beneath - up * overhead


def slab_of(corr, tile, depth):
    return jnp.where(tile % 2 == 0, corr, depth - 1 - corr)


def x_ring():
    depth, tiles = lax.axis_size("corr"), lax.axis_size("tx")
    order = []
    for tile in range(tiles):
        for q in range(depth):
            corr = q if tile % 2 == 0 else depth - 1 - q
            order.append(corr * tiles + tile)
    return order


def ring_halo(block, axes, order, dim, width):
    size = len(order)
    length = block.shape[dim]
    up = [(order[g], order[(g + 1) % size]) for g in range(size)]
    down = [(j, i) for i, j in up]
    last = lax.slice_in_dim(block, length - width, length, axis=dim)
    first = lax.slice_in_dim(block, 0, width, axis=dim)
    if size == 2:
        got = lax.ppermute(jnp.concatenate([first, last], dim), axes, up)
        after = lax.slice_in_dim(got, 0, width, axis=dim)
        before = lax.slice_in_dim(got, width, 2 * width, axis=dim)
        return before, after
    before = lax.ppermute(last, axes, up)
    after = lax.ppermute(first, axes, down)
    return before, after


def tendency(state, wind):
    west, east = ring_halo(state, ("corr", "tx"), x_ring(), 2, 2)
    south, north = ring_halo(state, ("ty",), list(range(lax.axis_size("ty"))), 3, 2)
    px = jnp.concatenate([west, state, east], 2)
    py = jnp.concatenate([south, state, north], 3)
    center = state
    far_x = px[:, :, :-4] - px[:, :, 4:]
    near_x = px[:, :, 3:-1] - px[:, :, 1:-3]
    far_sum_x = px[:, :, :-4] + px[:, :, 4:]
    near_sum_x = px[:, :, 3:-1] + px[:, :, 1:-3]
    far_y = py[:, :, :, :-4] - py[:, :, :, 4:]
    near_y = py[:, :, :, 3:-1] - py[:, :, :, 1:-3]
    far_sum_y = py[:, :, :, :-4] + py[:, :, :, 4:]
    near_sum_y = py[:, :, :, 3:-1] + py[:, :, :, 1:-3]
    laplace = 16.0 * (near_sum_x + near_sum_y) - (far_sum_x + far_sum_y) - 60.0 * center
    scale = jnp.array([0.5, 1.0], jnp.float32)[None, :, None, None, None] * (DT / 12.0)
    first = center[:, 0]
    second = center[:, 1]
    square_term = first * first * second
    react = jnp.stack(
        [A_RATE - (B_RATE + 1.0) * first + square_term, B_RATE * first - square_term], 1
    )
    flow = wind[0][None, None] * (far_x + 8.0 * near_x) + wind[1][None, None] * (
        far_y + 8.0 * near_y
    )
    return flow + scale * laplace + DT * react


def column_solve(rhs, inverse):
    return jnp.einsum(
        "lsxyk,sjk->lsxyj", rhs, inverse, precision=lax.Precision.HIGHEST
    )


def on_device(fields, wind, diffusion):
    inverse, upper, lower = vertical(diffusion)
    table = quad_cycle(STEPS)
    depth = lax.axis_size("corr")
    slab = fields.shape[1] // depth
    me = lax.axis_index("corr")
    tile = lax.axis_index("tx")
    start = slab_of(me, tile, depth) * slab
    own_fields = lax.dynamic_slice_in_dim(fields, start, slab, 1)
    own_wind = lax.dynamic_slice_in_dim(wind, start, slab, 1) * (-DT / 12.0)

    states = [own_fields] * depth
    e_hist = [dict() for _ in range(depth)]
    d_hist = [dict() for _ in range(depth)]
    g_now = [None] * depth
    for k in range(STEPS + depth - 1):
        active = [
            l for l in range(depth)
            if 0 <= k - l < STEPS or (k - l == STEPS and l < depth - 1)
        ]
        stacked = jnp.stack([states[l] for l in active], 0)
        own_e = tendency(stacked, own_wind)
        feeds = [l for l in active if l < depth - 1]
        if feeds:
            lows = [active.index(l) for l in feeds]
            lo, hi = lows[0], lows[-1] + 1
            own_g = vertical_apply(stacked[lo:hi], upper, lower)
            for i, l in enumerate(feeds):
                m = k - l
                g_now[l] = own_g[i]
                d_hist[l][m] = own_e[lo + i] - own_g[i]
        moving = [l for l in active if k - l < STEPS]
        rhs = []
        for l in moving:
            m = k - l
            i = active.index(l)
            e_hist[l][m] = own_e[i]
            total = states[l] + own_e[i]
            if l > 0:
                quad = None
                for slot in range(5):
                    node = m - 3 + slot
                    if node >= 0:
                        term = float(table[m, slot]) * d_hist[l - 1][node]
                        quad = term if quad is None else quad + term
                total = total + (quad + g_now[l - 1] - e_hist[l - 1][m])
            rhs.append(total)
        solved = column_solve(jnp.stack(rhs, 0), inverse)
        for i, l in enumerate(moving):
            states[l] = solved[i]
    out = jnp.zeros((1,) + own_fields.shape[:1] + fields.shape[1:], jnp.float32)
    out = lax.dynamic_update_slice_in_dim(
        out, jnp.stack(states, 0)[me][None], start, 2
    )
    for shift in range(1, depth):
        origin = (me - shift) % depth
        got = None
        for level in range(depth):
            pairs = [((level + shift) % depth, level)]
            arrived = lax.ppermute(states[level][None], "corr", pairs)
            got = arrived if got is None else jnp.where(me == level, arrived, got)
        out = lax.dynamic_update_slice_in_dim(
            out, got, slab_of(origin, tile, depth) * slab, 2
        )
    return out


def solution(mesh):
    placed = (P(None, "tx", "ty", None), P(None, "tx", "ty", None), P())
    return jax.shard_map(
        on_device,
        mesh=mesh,
        in_specs=placed,
        out_specs=P("corr", None, "tx", "ty", None),
        check_vma=False,
    )
```

```python
import jax
import jax.numpy as jnp
import numpy as np
from jax import lax
from jax.experimental import pallas as pl
from jax.experimental.pallas import tpu as pltpu
from jax.sharding import PartitionSpec as P

STEPS = 8


DT = 0.1
A_RATE = 1.0
B_RATE = 3.0


def quad_cycle(count):
    table = np.zeros((count, 5))
    for m in range(count):
        first = max(0, m - 3)
        nodes = [float(j - m) for j in range(first, m + 2)]
        for i, xi in enumerate(nodes):
            coeffs = [1.0]
            for xo in nodes:
                if xo != xi:
                    widened = [0.0] * (len(coeffs) + 1)
                    for k, c in enumerate(coeffs):
                        widened[k] = widened[k] - xo * c / (xi - xo)
                        widened[k + 1] = widened[k + 1] + c / (xi - xo)
                    coeffs = widened
            integral = 0.0
            for k, c in enumerate(coeffs):
                integral = integral + c / (k + 1)
            table[m, first + i - (m - 3)] = integral
    return table


def thomas_kernel(up_ref, low_ref, out_ref, c_ref, d_ref):
    n = out_ref.shape[0]
    shape = out_ref.shape[1:]
    lanes = lax.broadcasted_iota(jnp.int32, shape, 1)
    species = lax.broadcasted_iota(jnp.int32, shape, 0)
    zero = jnp.zeros(shape, jnp.float32)

    def column(ref, j):
        value = jnp.full(shape, ref[0, j], jnp.float32)
        for s in range(1, shape[0]):
            value = jnp.where(species == s, ref[s, j], value)
        return value

    def forward(j, carry):
        cprev, dprev = carry
        up = column(up_ref, j)
        low = column(low_ref, j)
        inv = 1.0 / ((1.0 + low + up) + low * cprev)
        c = -up * inv
        d = (jnp.where(lanes == j, 1.0, 0.0) + low * dprev) * inv
        c_ref[j] = c
        d_ref[j] = d
        return c, d

    lax.fori_loop(0, n, forward, (zero, zero), unroll=8)

    def backward(i, x):
        j = n - 1 - i
        x = d_ref[j] - c_ref[j] * x
        out_ref[j] = x
        return x

    lax.fori_loop(0, n, backward, zero, unroll=8)


def vertical(diffusion):
    species, depth = diffusion.shape
    keep = (jnp.arange(depth) < depth - 1).astype(jnp.float32)
    upper = diffusion * keep[None, :]
    lower = jnp.concatenate([jnp.zeros((species, 1), jnp.float32), upper[:, :-1]], 1)
    rows = pl.pallas_call(
        thomas_kernel,
        out_shape=jax.ShapeDtypeStruct((depth, species, depth), jnp.float32),
        in_specs=[pl.BlockSpec(memory_space=pltpu.SMEM)] * 2,
        scratch_shapes=[pltpu.VMEM((depth, species, depth), jnp.float32)] * 2,
        cost_estimate=pl.CostEstimate(
            flops=12 * depth * species * depth,
            transcendentals=0,
            bytes_accessed=4 * 2 * depth * species * depth,
        ),
    )(upper, lower)
    inverse = jnp.transpose(rows, (1, 0, 2))
    return (inverse, upper, lower)


def vertical_apply(w, upper, lower):
    zero_col = jnp.zeros(w.shape[:-1] + (1,), jnp.float32)
    beneath = jnp.concatenate([zero_col, w[..., :-1]], -1)
    overhead = jnp.concatenate([w[..., 1:], zero_col], -1)
    lo = lower[:, None, None, :]
    up = upper[:, None, None, :]
    return (lo + up) * w - lo * beneath - up * overhead


def slab_of(corr, tile, depth):
    return jnp.where(tile % 2 == 0, corr, depth - 1 - corr)


def x_ring():
    depth, tiles = lax.axis_size("corr"), lax.axis_size("tx")
    order = []
    for tile in range(tiles):
        for q in range(depth):
            corr = q if tile % 2 == 0 else depth - 1 - q
            order.append(corr * tiles + tile)
    return order


def ring_halo(block, axes, order, dim, width):
    size = len(order)
    length = block.shape[dim]
    up = [(order[g], order[(g + 1) % size]) for g in range(size)]
    down = [(j, i) for i, j in up]
    last = lax.slice_in_dim(block, length - width, length, axis=dim)
    first = lax.slice_in_dim(block, 0, width, axis=dim)
    before = lax.ppermute(last, axes, up)
    after = lax.ppermute(first, axes, down)
    return before, after


def tendency(state, wind):
    west, east = ring_halo(state, ("corr", "tx"), x_ring(), 2, 2)
    south, north = ring_halo(state, ("ty",), list(range(lax.axis_size("ty"))), 3, 2)
    px = jnp.concatenate([west, state, east], 2)
    py = jnp.concatenate([south, state, north], 3)
    center = state
    twelfth = 1.0 / 12.0
    far_x = px[:, :, :-4] - px[:, :, 4:]
    near_x = px[:, :, 3:-1] - px[:, :, 1:-3]
    far_sum_x = px[:, :, :-4] + px[:, :, 4:]
    near_sum_x = px[:, :, 3:-1] + px[:, :, 1:-3]
    far_y = py[:, :, :, :-4] - py[:, :, :, 4:]
    near_y = py[:, :, :, 3:-1] - py[:, :, :, 1:-3]
    far_sum_y = py[:, :, :, :-4] + py[:, :, :, 4:]
    near_sum_y = py[:, :, :, 3:-1] + py[:, :, :, 1:-3]
    dx1 = (far_x + 8.0 * near_x) * twelfth
    dy1 = (far_y + 8.0 * near_y) * twelfth
    laplace = (
        16.0 * (near_sum_x + near_sum_y) - (far_sum_x + far_sum_y) - 60.0 * center
    ) * twelfth
    kappa = jnp.array([0.5, 1.0], jnp.float32)[None, :, None, None, None]
    first = center[:, 0]
    second = center[:, 1]
    square_term = first * first * second
    react = jnp.stack(
        [A_RATE - (B_RATE + 1.0) * first + square_term, B_RATE * first - square_term], 1
    )
    flow = -(wind[0][None, None] * dx1 + wind[1][None, None] * dy1)
    return DT * (flow + kappa * laplace + react)


def column_solve(rhs, inverse):
    return jnp.einsum(
        "lsxyk,sjk->lsxyj", rhs, inverse, precision=lax.Precision.HIGHEST
    )


def on_device(fields, wind, diffusion):
    inverse, upper, lower = vertical(diffusion)
    table = quad_cycle(STEPS)
    depth = lax.axis_size("corr")
    slab = fields.shape[1] // depth
    me = lax.axis_index("corr")
    tile = lax.axis_index("tx")
    start = slab_of(me, tile, depth) * slab
    own_fields = lax.dynamic_slice_in_dim(fields, start, slab, 1)
    own_wind = lax.dynamic_slice_in_dim(wind, start, slab, 1)

    states = [own_fields] * depth
    e_hist = [dict() for _ in range(depth)]
    d_hist = [dict() for _ in range(depth)]
    g_now = [None] * depth
    for k in range(STEPS + depth - 1):
        active = [
            l for l in range(depth)
            if 0 <= k - l < STEPS or (k - l == STEPS and l < depth - 1)
        ]
        stacked = jnp.stack([states[l] for l in active], 0)
        own_e = tendency(stacked, own_wind)
        feeds = [l for l in active if l < depth - 1]
        if feeds:
            lows = [active.index(l) for l in feeds]
            lo, hi = lows[0], lows[-1] + 1
            own_g = vertical_apply(stacked[lo:hi], upper, lower)
            for i, l in enumerate(feeds):
                m = k - l
                g_now[l] = own_g[i]
                d_hist[l][m] = own_e[lo + i] - own_g[i]
        moving = [l for l in active if k - l < STEPS]
        rhs = []
        for l in moving:
            m = k - l
            i = active.index(l)
            e_hist[l][m] = own_e[i]
            total = states[l] + own_e[i]
            if l > 0:
                quad = None
                for slot in range(5):
                    node = m - 3 + slot
                    if node >= 0:
                        term = float(table[m, slot]) * d_hist[l - 1][node]
                        quad = term if quad is None else quad + term
                total = total + (quad + g_now[l - 1] - e_hist[l - 1][m])
            rhs.append(total)
        solved = column_solve(jnp.stack(rhs, 0), inverse)
        for i, l in enumerate(moving):
            states[l] = solved[i]
    out = jnp.zeros((1,) + own_fields.shape[:1] + fields.shape[1:], jnp.float32)
    out = lax.dynamic_update_slice_in_dim(
        out, jnp.stack(states, 0)[me][None], start, 2
    )
    for shift in range(1, depth):
        origin = (me - shift) % depth
        got = None
        for level in range(depth):
            pairs = [((level + shift) % depth, level)]
            arrived = lax.ppermute(states[level][None], "corr", pairs)
            got = arrived if got is None else jnp.where(me == level, arrived, got)
        out = lax.dynamic_update_slice_in_dim(
            out, got, slab_of(origin, tile, depth) * slab, 2
        )
    return out


def solution(mesh):
    placed = (P(None, "tx", "ty", None), P(None, "tx", "ty", None), P())
    return jax.shard_map(
        on_device,
        mesh=mesh,
        in_specs=placed,
        out_specs=P("corr", None, "tx", "ty", None),
        check_vma=False,
    )
```

```python
import jax
import jax.numpy as jnp
import numpy as np
from jax import lax
from jax.experimental import pallas as pl
from jax.experimental.pallas import tpu as pltpu
from jax.sharding import PartitionSpec as P

STEPS = 8


DT = 0.1
A_RATE = 1.0
B_RATE = 3.0


def quad_cycle(count):
    table = np.zeros((count, 5))
    for m in range(count):
        first = max(0, m - 3)
        nodes = [float(j - m) for j in range(first, m + 2)]
        for i, xi in enumerate(nodes):
            coeffs = [1.0]
            for xo in nodes:
                if xo != xi:
                    widened = [0.0] * (len(coeffs) + 1)
                    for k, c in enumerate(coeffs):
                        widened[k] = widened[k] - xo * c / (xi - xo)
                        widened[k + 1] = widened[k + 1] + c / (xi - xo)
                    coeffs = widened
            integral = 0.0
            for k, c in enumerate(coeffs):
                integral = integral + c / (k + 1)
            table[m, first + i - (m - 3)] = integral
    return table


def thomas_kernel(up_ref, low_ref, out_ref, c_ref, d_ref):
    n = out_ref.shape[0]
    shape = out_ref.shape[1:]
    lanes = lax.broadcasted_iota(jnp.int32, shape, 1)
    species = lax.broadcasted_iota(jnp.int32, shape, 0)
    zero = jnp.zeros(shape, jnp.float32)

    def column(ref, j):
        value = jnp.full(shape, ref[0, j], jnp.float32)
        for s in range(1, shape[0]):
            value = jnp.where(species == s, ref[s, j], value)
        return value

    def forward(j, carry):
        cprev, dprev = carry
        up = column(up_ref, j)
        low = column(low_ref, j)
        inv = 1.0 / ((1.0 + low + up) + low * cprev)
        c = -up * inv
        d = (jnp.where(lanes == j, 1.0, 0.0) + low * dprev) * inv
        c_ref[j] = c
        d_ref[j] = d
        return c, d

    lax.fori_loop(0, n, forward, (zero, zero), unroll=8)

    def backward(i, x):
        j = n - 1 - i
        x = d_ref[j] - c_ref[j] * x
        out_ref[j] = x
        return x

    lax.fori_loop(0, n, backward, zero, unroll=8)


def vertical(diffusion):
    species, depth = diffusion.shape
    keep = (jnp.arange(depth) < depth - 1).astype(jnp.float32)
    upper = diffusion * keep[None, :]
    lower = jnp.concatenate([jnp.zeros((species, 1), jnp.float32), upper[:, :-1]], 1)
    rows = pl.pallas_call(
        thomas_kernel,
        out_shape=jax.ShapeDtypeStruct((depth, species, depth), jnp.float32),
        in_specs=[pl.BlockSpec(memory_space=pltpu.SMEM)] * 2,
        scratch_shapes=[pltpu.VMEM((depth, species, depth), jnp.float32)] * 2,
        cost_estimate=pl.CostEstimate(
            flops=12 * depth * species * depth,
            transcendentals=0,
            bytes_accessed=4 * 2 * depth * species * depth,
        ),
    )(upper, lower)
    inverse = jnp.transpose(rows, (1, 0, 2))
    return (inverse, upper, lower)


def vertical_apply(w, upper, lower):
    zero_col = jnp.zeros(w.shape[:-1] + (1,), jnp.float32)
    beneath = jnp.concatenate([zero_col, w[..., :-1]], -1)
    overhead = jnp.concatenate([w[..., 1:], zero_col], -1)
    lo = lower[:, None, None, :]
    up = upper[:, None, None, :]
    return (lo + up) * w - lo * beneath - up * overhead


def slab_of(corr, tile, depth):
    return jnp.where(tile % 2 == 0, corr, depth - 1 - corr)


def x_ring():
    depth, tiles = lax.axis_size("corr"), lax.axis_size("tx")
    order = []
    for tile in range(tiles):
        for q in range(depth):
            corr = q if tile % 2 == 0 else depth - 1 - q
            order.append(corr * tiles + tile)
    return order


def ring_halo(block, axes, order, dim, width):
    size = len(order)
    length = block.shape[dim]
    up = [(order[g], order[(g + 1) % size]) for g in range(size)]
    down = [(j, i) for i, j in up]
    last = lax.slice_in_dim(block, length - width, length, axis=dim)
    first = lax.slice_in_dim(block, 0, width, axis=dim)
    if size == 2:
        got = lax.ppermute(jnp.concatenate([first, last], dim), axes, up)
        after = lax.slice_in_dim(got, 0, width, axis=dim)
        before = lax.slice_in_dim(got, width, 2 * width, axis=dim)
        return before, after
    before = lax.ppermute(last, axes, up)
    after = lax.ppermute(first, axes, down)
    return before, after


def swap_halo(block, axes, order, parity, dim, width):
    size = len(order)
    length = block.shape[dim]
    last = lax.slice_in_dim(block, length - width, length, axis=dim)
    first = lax.slice_in_dim(block, 0, width, axis=dim)
    got = []
    for offset in range(2):
        pairs = []
        for g in range(offset, size, 2):
            pairs += [(order[g], order[(g + 1) % size]), (order[(g + 1) % size], order[g])]
        sent = jnp.where(parity == offset, last, first)
        got.append(lax.ppermute(sent, axes, pairs))
    before = jnp.where(parity == 0, got[1], got[0])
    after = jnp.where(parity == 0, got[0], got[1])
    return before, after


def tendency(state, wind, parity):
    ring = x_ring()
    if len(ring) % 2 == 0:
        west, east = swap_halo(state, ("corr", "tx"), ring, parity, 2, 2)
    else:
        west, east = ring_halo(state, ("corr", "tx"), ring, 2, 2)
    south, north = ring_halo(state, ("ty",), list(range(lax.axis_size("ty"))), 3, 2)
    px = jnp.concatenate([west, state, east], 2)
    py = jnp.concatenate([south, state, north], 3)
    center = state
    twelfth = 1.0 / 12.0
    far_x = px[:, :, :-4] - px[:, :, 4:]
    near_x = px[:, :, 3:-1] - px[:, :, 1:-3]
    far_sum_x = px[:, :, :-4] + px[:, :, 4:]
    near_sum_x = px[:, :, 3:-1] + px[:, :, 1:-3]
    far_y = py[:, :, :, :-4] - py[:, :, :, 4:]
    near_y = py[:, :, :, 3:-1] - py[:, :, :, 1:-3]
    far_sum_y = py[:, :, :, :-4] + py[:, :, :, 4:]
    near_sum_y = py[:, :, :, 3:-1] + py[:, :, :, 1:-3]
    dx1 = (far_x + 8.0 * near_x) * twelfth
    dy1 = (far_y + 8.0 * near_y) * twelfth
    laplace = (
        16.0 * (near_sum_x + near_sum_y) - (far_sum_x + far_sum_y) - 60.0 * center
    ) * twelfth
    kappa = jnp.array([0.5, 1.0], jnp.float32)[None, :, None, None, None]
    first = center[:, 0]
    second = center[:, 1]
    square_term = first * first * second
    react = jnp.stack(
        [A_RATE - (B_RATE + 1.0) * first + square_term, B_RATE * first - square_term], 1
    )
    flow = -(wind[0][None, None] * dx1 + wind[1][None, None] * dy1)
    return DT * (flow + kappa * laplace + react)


def column_solve(rhs, inverse):
    return jnp.einsum(
        "lsxyk,sjk->lsxyj", rhs, inverse, precision=lax.Precision.HIGHEST
    )


def on_device(fields, wind, diffusion):
    inverse, upper, lower = vertical(diffusion)
    table = quad_cycle(STEPS)
    depth = lax.axis_size("corr")
    slab = fields.shape[1] // depth
    me = lax.axis_index("corr")
    tile = lax.axis_index("tx")
    start = slab_of(me, tile, depth) * slab
    parity = (tile * depth + slab_of(me, tile, depth)) % 2
    own_fields = lax.dynamic_slice_in_dim(fields, start, slab, 1)
    own_wind = lax.dynamic_slice_in_dim(wind, start, slab, 1)

    states = [own_fields] * depth
    e_hist = [dict() for _ in range(depth)]
    d_hist = [dict() for _ in range(depth)]
    g_now = [None] * depth
    for k in range(STEPS + depth - 1):
        active = [
            l for l in range(depth)
            if 0 <= k - l < STEPS or (k - l == STEPS and l < depth - 1)
        ]
        stacked = jnp.stack([states[l] for l in active], 0)
        own_e = tendency(stacked, own_wind, parity)
        feeds = [l for l in active if l < depth - 1]
        if feeds:
            lows = [active.index(l) for l in feeds]
            lo, hi = lows[0], lows[-1] + 1
            own_g = vertical_apply(stacked[lo:hi], upper, lower)
            for i, l in enumerate(feeds):
                m = k - l
                g_now[l] = own_g[i]
                d_hist[l][m] = own_e[lo + i] - own_g[i]
        moving = [l for l in active if k - l < STEPS]
        rhs = []
        for l in moving:
            m = k - l
            i = active.index(l)
            e_hist[l][m] = own_e[i]
            total = states[l] + own_e[i]
            if l > 0:
                quad = None
                for slot in range(5):
                    node = m - 3 + slot
                    if node >= 0:
                        term = float(table[m, slot]) * d_hist[l - 1][node]
                        quad = term if quad is None else quad + term
                total = total + (quad + g_now[l - 1] - e_hist[l - 1][m])
            rhs.append(total)
        solved = column_solve(jnp.stack(rhs, 0), inverse)
        for i, l in enumerate(moving):
            states[l] = solved[i]
    out = jnp.zeros((1,) + own_fields.shape[:1] + fields.shape[1:], jnp.float32)
    out = lax.dynamic_update_slice_in_dim(
        out, jnp.stack(states, 0)[me][None], start, 2
    )
    for shift in range(1, depth):
        origin = (me - shift) % depth
        got = None
        for level in range(depth):
            pairs = [((level + shift) % depth, level)]
            arrived = lax.ppermute(states[level][None], "corr", pairs)
            got = arrived if got is None else jnp.where(me == level, arrived, got)
        out = lax.dynamic_update_slice_in_dim(
            out, got, slab_of(origin, tile, depth) * slab, 2
        )
    return out


def solution(mesh):
    placed = (P(None, "tx", "ty", None), P(None, "tx", "ty", None), P())
    return jax.shard_map(
        on_device,
        mesh=mesh,
        in_specs=placed,
        out_specs=P("corr", None, "tx", "ty", None),
        check_vma=False,
    )
```

```python
import jax
import jax.numpy as jnp
import numpy as np
from jax import lax
from jax.experimental import pallas as pl
from jax.experimental.pallas import tpu as pltpu
from jax.sharding import PartitionSpec as P

STEPS = 8


DT = 0.1
A_RATE = 1.0
B_RATE = 3.0


def quad_cycle(count):
    table = np.zeros((count, 5))
    for m in range(count):
        first = max(0, m - 3)
        nodes = [float(j - m) for j in range(first, m + 2)]
        for i, xi in enumerate(nodes):
            coeffs = [1.0]
            for xo in nodes:
                if xo != xi:
                    widened = [0.0] * (len(coeffs) + 1)
                    for k, c in enumerate(coeffs):
                        widened[k] = widened[k] - xo * c / (xi - xo)
                        widened[k + 1] = widened[k + 1] + c / (xi - xo)
                    coeffs = widened
            integral = 0.0
            for k, c in enumerate(coeffs):
                integral = integral + c / (k + 1)
            table[m, first + i - (m - 3)] = integral
    return table


def thomas_kernel(diff_ref, out_ref, c_ref, d_ref):
    n = out_ref.shape[0]
    shape = out_ref.shape[1:]
    lanes = lax.broadcasted_iota(jnp.int32, shape, 1)
    species = lax.broadcasted_iota(jnp.int32, shape, 0)
    zero = jnp.zeros(shape, jnp.float32)

    def column(j):
        value = jnp.full(shape, diff_ref[0, j], jnp.float32)
        for s in range(1, shape[0]):
            value = jnp.where(species == s, diff_ref[s, j], value)
        return value

    def forward(j, carry):
        cprev, dprev = carry
        up = jnp.where(j < n - 1, column(j), 0.0)
        low = jnp.where(j > 0, column(jnp.maximum(j - 1, 0)), 0.0)
        inv = 1.0 / ((1.0 + low + up) + low * cprev)
        c = -up * inv
        d = (jnp.where(lanes == j, 1.0, 0.0) + low * dprev) * inv
        c_ref[j] = c
        d_ref[j] = d
        return c, d

    lax.fori_loop(0, n, forward, (zero, zero), unroll=8)

    def backward(i, x):
        j = n - 1 - i
        x = d_ref[j] - c_ref[j] * x
        out_ref[j] = x
        return x

    lax.fori_loop(0, n, backward, zero, unroll=8)


def vertical(diffusion):
    species, depth = diffusion.shape
    keep = (jnp.arange(depth) < depth - 1).astype(jnp.float32)
    upper = diffusion * keep[None, :]
    lower = jnp.concatenate([jnp.zeros((species, 1), jnp.float32), upper[:, :-1]], 1)
    rows = pl.pallas_call(
        thomas_kernel,
        out_shape=jax.ShapeDtypeStruct((depth, species, depth), jnp.float32),
        in_specs=[pl.BlockSpec(memory_space=pltpu.SMEM)],
        scratch_shapes=[pltpu.VMEM((depth, species, depth), jnp.float32)] * 2,
        cost_estimate=pl.CostEstimate(
            flops=12 * depth * species * depth,
            transcendentals=0,
            bytes_accessed=4 * 2 * depth * species * depth,
        ),
    )(diffusion)
    inverse = jnp.transpose(rows, (1, 0, 2))
    return (inverse, upper, lower)


def vertical_apply(w, upper, lower):
    zero_col = jnp.zeros(w.shape[:-1] + (1,), jnp.float32)
    beneath = jnp.concatenate([zero_col, w[..., :-1]], -1)
    overhead = jnp.concatenate([w[..., 1:], zero_col], -1)
    lo = lower[:, None, None, :]
    up = upper[:, None, None, :]
    return (lo + up) * w - lo * beneath - up * overhead


def slab_of(corr, tile, depth):
    return jnp.where(tile % 2 == 0, corr, depth - 1 - corr)


def x_ring():
    depth, tiles = lax.axis_size("corr"), lax.axis_size("tx")
    order = []
    for tile in range(tiles):
        for q in range(depth):
            corr = q if tile % 2 == 0 else depth - 1 - q
            order.append(corr * tiles + tile)
    return order


def ring_halo(block, axes, order, dim, width):
    size = len(order)
    length = block.shape[dim]
    up = [(order[g], order[(g + 1) % size]) for g in range(size)]
    down = [(j, i) for i, j in up]
    last = lax.slice_in_dim(block, length - width, length, axis=dim)
    first = lax.slice_in_dim(block, 0, width, axis=dim)
    if size == 2:
        got = lax.ppermute(jnp.concatenate([first, last], dim), axes, up)
        after = lax.slice_in_dim(got, 0, width, axis=dim)
        before = lax.slice_in_dim(got, width, 2 * width, axis=dim)
        return before, after
    before = lax.ppermute(last, axes, up)
    after = lax.ppermute(first, axes, down)
    return before, after


def swap_halo(block, axes, order, parity, dim, width):
    size = len(order)
    length = block.shape[dim]
    last = lax.slice_in_dim(block, length - width, length, axis=dim)
    first = lax.slice_in_dim(block, 0, width, axis=dim)
    got = []
    for offset in range(2):
        pairs = []
        for g in range(offset, size, 2):
            pairs += [(order[g], order[(g + 1) % size]), (order[(g + 1) % size], order[g])]
        sent = jnp.where(parity == offset, last, first)
        got.append(lax.ppermute(sent, axes, pairs))
    before = jnp.where(parity == 0, got[1], got[0])
    after = jnp.where(parity == 0, got[0], got[1])
    return before, after


def tendency(state, wind, parity):
    ring = x_ring()
    if len(ring) % 2 == 0:
        west, east = swap_halo(state, ("corr", "tx"), ring, parity, 2, 2)
    else:
        west, east = ring_halo(state, ("corr", "tx"), ring, 2, 2)
    south, north = ring_halo(state, ("ty",), list(range(lax.axis_size("ty"))), 3, 2)
    px = jnp.concatenate([west, state, east], 2)
    py = jnp.concatenate([south, state, north], 3)
    center = state
    twelfth = 1.0 / 12.0
    far_x = px[:, :, :-4] - px[:, :, 4:]
    near_x = px[:, :, 3:-1] - px[:, :, 1:-3]
    far_sum_x = px[:, :, :-4] + px[:, :, 4:]
    near_sum_x = px[:, :, 3:-1] + px[:, :, 1:-3]
    far_y = py[:, :, :, :-4] - py[:, :, :, 4:]
    near_y = py[:, :, :, 3:-1] - py[:, :, :, 1:-3]
    far_sum_y = py[:, :, :, :-4] + py[:, :, :, 4:]
    near_sum_y = py[:, :, :, 3:-1] + py[:, :, :, 1:-3]
    dx1 = (far_x + 8.0 * near_x) * twelfth
    dy1 = (far_y + 8.0 * near_y) * twelfth
    laplace = (
        16.0 * (near_sum_x + near_sum_y) - (far_sum_x + far_sum_y) - 60.0 * center
    ) * twelfth
    kappa = jnp.array([0.5, 1.0], jnp.float32)[None, :, None, None, None]
    first = center[:, 0]
    second = center[:, 1]
    square_term = first * first * second
    react = jnp.stack(
        [A_RATE - (B_RATE + 1.0) * first + square_term, B_RATE * first - square_term], 1
    )
    flow = -(wind[0][None, None] * dx1 + wind[1][None, None] * dy1)
    return DT * (flow + kappa * laplace + react)


def column_solve(rhs, inverse):
    return jnp.einsum(
        "lsxyk,sjk->lsxyj", rhs, inverse, precision=lax.Precision.HIGHEST
    )


def on_device(fields, wind, diffusion):
    inverse, upper, lower = vertical(diffusion)
    table = quad_cycle(STEPS)
    depth = lax.axis_size("corr")
    slab = fields.shape[1] // depth
    me = lax.axis_index("corr")
    tile = lax.axis_index("tx")
    start = slab_of(me, tile, depth) * slab
    parity = (tile * depth + slab_of(me, tile, depth)) % 2
    own_fields = lax.dynamic_slice_in_dim(fields, start, slab, 1)
    own_wind = lax.dynamic_slice_in_dim(wind, start, slab, 1)

    states = [own_fields] * depth
    e_hist = [dict() for _ in range(depth)]
    d_hist = [dict() for _ in range(depth)]
    g_now = [None] * depth
    for k in range(STEPS + depth - 1):
        active = [
            l for l in range(depth)
            if 0 <= k - l < STEPS or (k - l == STEPS and l < depth - 1)
        ]
        stacked = jnp.stack([states[l] for l in active], 0)
        own_e = tendency(stacked, own_wind, parity)
        feeds = [l for l in active if l < depth - 1]
        if feeds:
            lows = [active.index(l) for l in feeds]
            lo, hi = lows[0], lows[-1] + 1
            own_g = vertical_apply(stacked[lo:hi], upper, lower)
            for i, l in enumerate(feeds):
                m = k - l
                g_now[l] = own_g[i]
                d_hist[l][m] = own_e[lo + i] - own_g[i]
        moving = [l for l in active if k - l < STEPS]
        rhs = []
        for l in moving:
            m = k - l
            i = active.index(l)
            e_hist[l][m] = own_e[i]
            total = states[l] + own_e[i]
            if l > 0:
                quad = None
                for slot in range(5):
                    node = m - 3 + slot
                    if node >= 0:
                        term = float(table[m, slot]) * d_hist[l - 1][node]
                        quad = term if quad is None else quad + term
                total = total + (quad + g_now[l - 1] - e_hist[l - 1][m])
            rhs.append(total)
        solved = column_solve(jnp.stack(rhs, 0), inverse)
        for i, l in enumerate(moving):
            states[l] = solved[i]
    out = jnp.zeros((1,) + own_fields.shape[:1] + fields.shape[1:], jnp.float32)
    out = lax.dynamic_update_slice_in_dim(
        out, jnp.stack(states, 0)[me][None], start, 2
    )
    for shift in range(1, depth):
        origin = (me - shift) % depth
        got = None
        for level in range(depth):
            pairs = [((level + shift) % depth, level)]
            arrived = lax.ppermute(states[level][None], "corr", pairs)
            got = arrived if got is None else jnp.where(me == level, arrived, got)
        out = lax.dynamic_update_slice_in_dim(
            out, got, slab_of(origin, tile, depth) * slab, 2
        )
    return out


def solution(mesh):
    placed = (P(None, "tx", "ty", None), P(None, "tx", "ty", None), P())
    return jax.shard_map(
        on_device,
        mesh=mesh,
        in_specs=placed,
        out_specs=P("corr", None, "tx", "ty", None),
        check_vma=False,
    )
```

```python
import jax
import jax.numpy as jnp
import numpy as np
from jax import lax
from jax.experimental import pallas as pl
from jax.experimental.pallas import tpu as pltpu
from jax.sharding import PartitionSpec as P

STEPS = 8


DT = 0.1
A_RATE = 1.0
B_RATE = 3.0


def quad_cycle(count):
    table = np.zeros((count, 5))
    for m in range(count):
        first = max(0, m - 3)
        nodes = [float(j - m) for j in range(first, m + 2)]
        for i, xi in enumerate(nodes):
            coeffs = [1.0]
            for xo in nodes:
                if xo != xi:
                    widened = [0.0] * (len(coeffs) + 1)
                    for k, c in enumerate(coeffs):
                        widened[k] = widened[k] - xo * c / (xi - xo)
                        widened[k + 1] = widened[k + 1] + c / (xi - xo)
                    coeffs = widened
            integral = 0.0
            for k, c in enumerate(coeffs):
                integral = integral + c / (k + 1)
            table[m, first + i - (m - 3)] = integral
    return table


def thomas_kernel(diff_ref, out_ref, c_ref, d_ref):
    n = out_ref.shape[0]
    shape = out_ref.shape[1:]
    lanes = lax.broadcasted_iota(jnp.int32, shape, 1)
    species = lax.broadcasted_iota(jnp.int32, shape, 0)
    zero = jnp.zeros(shape, jnp.float32)

    def column(j):
        value = jnp.full(shape, diff_ref[0, j], jnp.float32)
        for s in range(1, shape[0]):
            value = jnp.where(species == s, diff_ref[s, j], value)
        return value

    def forward(j, carry):
        cprev, dprev = carry
        up = jnp.where(j < n - 1, column(j), 0.0)
        low = jnp.where(j > 0, column(jnp.maximum(j - 1, 0)), 0.0)
        inv = 1.0 / ((1.0 + low + up) + low * cprev)
        c = -up * inv
        d = (jnp.where(lanes == j, 1.0, 0.0) + low * dprev) * inv
        c_ref[j] = c
        d_ref[j] = d
        return c, d

    lax.fori_loop(0, n, forward, (zero, zero), unroll=16)

    def backward(i, x):
        j = n - 1 - i
        x = d_ref[j] - c_ref[j] * x
        out_ref[j] = x
        return x

    lax.fori_loop(0, n, backward, zero, unroll=16)


def vertical(diffusion):
    species, depth = diffusion.shape
    keep = (jnp.arange(depth) < depth - 1).astype(jnp.float32)
    upper = diffusion * keep[None, :]
    lower = jnp.concatenate([jnp.zeros((species, 1), jnp.float32), upper[:, :-1]], 1)
    rows = pl.pallas_call(
        thomas_kernel,
        out_shape=jax.ShapeDtypeStruct((depth, species, depth), jnp.float32),
        in_specs=[pl.BlockSpec(memory_space=pltpu.SMEM)],
        scratch_shapes=[pltpu.VMEM((depth, species, depth), jnp.float32)] * 2,
        cost_estimate=pl.CostEstimate(
            flops=12 * depth * species * depth,
            transcendentals=0,
            bytes_accessed=4 * 2 * depth * species * depth,
        ),
    )(diffusion)
    inverse = jnp.transpose(rows, (1, 0, 2))
    return (inverse, upper, lower)


def vertical_apply(w, upper, lower):
    zero_col = jnp.zeros(w.shape[:-1] + (1,), jnp.float32)
    beneath = jnp.concatenate([zero_col, w[..., :-1]], -1)
    overhead = jnp.concatenate([w[..., 1:], zero_col], -1)
    lo = lower[:, None, None, :]
    up = upper[:, None, None, :]
    return (lo + up) * w - lo * beneath - up * overhead


def slab_of(corr, tile, depth):
    return jnp.where(tile % 2 == 0, corr, depth - 1 - corr)


def x_ring():
    depth, tiles = lax.axis_size("corr"), lax.axis_size("tx")
    order = []
    for tile in range(tiles):
        for q in range(depth):
            corr = q if tile % 2 == 0 else depth - 1 - q
            order.append(corr * tiles + tile)
    return order


def ring_halo(block, axes, order, dim, width):
    size = len(order)
    length = block.shape[dim]
    up = [(order[g], order[(g + 1) % size]) for g in range(size)]
    down = [(j, i) for i, j in up]
    last = lax.slice_in_dim(block, length - width, length, axis=dim)
    first = lax.slice_in_dim(block, 0, width, axis=dim)
    if size == 2:
        got = lax.ppermute(jnp.concatenate([first, last], dim), axes, up)
        after = lax.slice_in_dim(got, 0, width, axis=dim)
        before = lax.slice_in_dim(got, width, 2 * width, axis=dim)
        return before, after
    before = lax.ppermute(last, axes, up)
    after = lax.ppermute(first, axes, down)
    return before, after


def swap_halo(block, axes, order, parity, dim, width):
    size = len(order)
    length = block.shape[dim]
    last = lax.slice_in_dim(block, length - width, length, axis=dim)
    first = lax.slice_in_dim(block, 0, width, axis=dim)
    got = []
    for offset in range(2):
        pairs = []
        for g in range(offset, size, 2):
            pairs += [(order[g], order[(g + 1) % size]), (order[(g + 1) % size], order[g])]
        sent = jnp.where(parity == offset, last, first)
        got.append(lax.ppermute(sent, axes, pairs))
    before = jnp.where(parity == 0, got[1], got[0])
    after = jnp.where(parity == 0, got[0], got[1])
    return before, after


def tendency(state, wind, parity):
    ring = x_ring()
    if len(ring) % 2 == 0:
        west, east = swap_halo(state, ("corr", "tx"), ring, parity, 2, 2)
    else:
        west, east = ring_halo(state, ("corr", "tx"), ring, 2, 2)
    south, north = ring_halo(state, ("ty",), list(range(lax.axis_size("ty"))), 3, 2)
    px = jnp.concatenate([west, state, east], 2)
    py = jnp.concatenate([south, state, north], 3)
    center = state
    twelfth = 1.0 / 12.0
    far_x = px[:, :, :-4] - px[:, :, 4:]
    near_x = px[:, :, 3:-1] - px[:, :, 1:-3]
    far_sum_x = px[:, :, :-4] + px[:, :, 4:]
    near_sum_x = px[:, :, 3:-1] + px[:, :, 1:-3]
    far_y = py[:, :, :, :-4] - py[:, :, :, 4:]
    near_y = py[:, :, :, 3:-1] - py[:, :, :, 1:-3]
    far_sum_y = py[:, :, :, :-4] + py[:, :, :, 4:]
    near_sum_y = py[:, :, :, 3:-1] + py[:, :, :, 1:-3]
    dx1 = (far_x + 8.0 * near_x) * twelfth
    dy1 = (far_y + 8.0 * near_y) * twelfth
    laplace = (
        16.0 * (near_sum_x + near_sum_y) - (far_sum_x + far_sum_y) - 60.0 * center
    ) * twelfth
    kappa = jnp.array([0.5, 1.0], jnp.float32)[None, :, None, None, None]
    first = center[:, 0]
    second = center[:, 1]
    square_term = first * first * second
    react = jnp.stack(
        [A_RATE - (B_RATE + 1.0) * first + square_term, B_RATE * first - square_term], 1
    )
    flow = -(wind[0][None, None] * dx1 + wind[1][None, None] * dy1)
    return DT * (flow + kappa * laplace + react)


def column_solve(rhs, inverse):
    return jnp.einsum(
        "lsxyk,sjk->lsxyj", rhs, inverse, precision=lax.Precision.HIGHEST
    )


def on_device(fields, wind, diffusion):
    inverse, upper, lower = vertical(diffusion)
    table = quad_cycle(STEPS)
    depth = lax.axis_size("corr")
    slab = fields.shape[1] // depth
    me = lax.axis_index("corr")
    tile = lax.axis_index("tx")
    start = slab_of(me, tile, depth) * slab
    parity = (tile * depth + slab_of(me, tile, depth)) % 2
    own_fields = lax.dynamic_slice_in_dim(fields, start, slab, 1)
    own_wind = lax.dynamic_slice_in_dim(wind, start, slab, 1)

    states = [own_fields] * depth
    e_hist = [dict() for _ in range(depth)]
    d_hist = [dict() for _ in range(depth)]
    g_now = [None] * depth
    for k in range(STEPS + depth - 1):
        active = [
            l for l in range(depth)
            if 0 <= k - l < STEPS or (k - l == STEPS and l < depth - 1)
        ]
        stacked = jnp.stack([states[l] for l in active], 0)
        own_e = tendency(stacked, own_wind, parity)
        feeds = [l for l in active if l < depth - 1]
        if feeds:
            lows = [active.index(l) for l in feeds]
            lo, hi = lows[0], lows[-1] + 1
            own_g = vertical_apply(stacked[lo:hi], upper, lower)
            for i, l in enumerate(feeds):
                m = k - l
                g_now[l] = own_g[i]
                d_hist[l][m] = own_e[lo + i] - own_g[i]
        moving = [l for l in active if k - l < STEPS]
        rhs = []
        for l in moving:
            m = k - l
            i = active.index(l)
            e_hist[l][m] = own_e[i]
            total = states[l] + own_e[i]
            if l > 0:
                quad = None
                for slot in range(5):
                    node = m - 3 + slot
                    if node >= 0:
                        term = float(table[m, slot]) * d_hist[l - 1][node]
                        quad = term if quad is None else quad + term
                total = total + (quad + g_now[l - 1] - e_hist[l - 1][m])
            rhs.append(total)
        solved = column_solve(jnp.stack(rhs, 0), inverse)
        for i, l in enumerate(moving):
            states[l] = solved[i]
    out = jnp.zeros((1,) + own_fields.shape[:1] + fields.shape[1:], jnp.float32)
    out = lax.dynamic_update_slice_in_dim(
        out, jnp.stack(states, 0)[me][None], start, 2
    )
    for shift in range(1, depth):
        origin = (me - shift) % depth
        got = None
        for level in range(depth):
            pairs = [((level + shift) % depth, level)]
            arrived = lax.ppermute(states[level][None], "corr", pairs)
            got = arrived if got is None else jnp.where(me == level, arrived, got)
        out = lax.dynamic_update_slice_in_dim(
            out, got, slab_of(origin, tile, depth) * slab, 2
        )
    return out


def solution(mesh):
    placed = (P(None, "tx", "ty", None), P(None, "tx", "ty", None), P())
    return jax.shard_map(
        on_device,
        mesh=mesh,
        in_specs=placed,
        out_specs=P("corr", None, "tx", "ty", None),
        check_vma=False,
    )
```

```python
import jax
import jax.numpy as jnp
import numpy as np
from jax import lax
from jax.experimental import pallas as pl
from jax.experimental.pallas import tpu as pltpu
from jax.sharding import PartitionSpec as P

STEPS = 8


DT = 0.1
A_RATE = 1.0
B_RATE = 3.0


def quad_cycle(count):
    table = np.zeros((count, 5))
    for m in range(count):
        first = max(0, m - 3)
        nodes = [float(j - m) for j in range(first, m + 2)]
        for i, xi in enumerate(nodes):
            coeffs = [1.0]
            for xo in nodes:
                if xo != xi:
                    widened = [0.0] * (len(coeffs) + 1)
                    for k, c in enumerate(coeffs):
                        widened[k] = widened[k] - xo * c / (xi - xo)
                        widened[k + 1] = widened[k + 1] + c / (xi - xo)
                    coeffs = widened
            integral = 0.0
            for k, c in enumerate(coeffs):
                integral = integral + c / (k + 1)
            table[m, first + i - (m - 3)] = integral
    return table


def thomas_kernel(diff_ref, out_ref, c_ref, d_ref):
    n = out_ref.shape[0]
    shape = out_ref.shape[1:]
    lanes = lax.broadcasted_iota(jnp.int32, shape, 1)
    species = lax.broadcasted_iota(jnp.int32, shape, 0)
    zero = jnp.zeros(shape, jnp.float32)

    def column(j):
        value = jnp.full(shape, diff_ref[0, j], jnp.float32)
        for s in range(1, shape[0]):
            value = jnp.where(species == s, diff_ref[s, j], value)
        return value

    def forward(j, carry):
        cprev, dprev = carry
        up = jnp.where(j < n - 1, column(j), 0.0)
        low = jnp.where(j > 0, column(jnp.maximum(j - 1, 0)), 0.0)
        inv = 1.0 / ((1.0 + low + up) + low * cprev)
        c = -up * inv
        d = (jnp.where(lanes == j, 1.0, 0.0) + low * dprev) * inv
        c_ref[j] = c
        d_ref[j] = d
        return c, d

    lax.fori_loop(0, n, forward, (zero, zero), unroll=16)

    def backward(i, x):
        j = n - 1 - i
        x = d_ref[j] - c_ref[j] * x
        out_ref[j] = x
        return x

    lax.fori_loop(0, n, backward, zero, unroll=16)


def vertical(diffusion):
    species, depth = diffusion.shape
    keep = (jnp.arange(depth) < depth - 1).astype(jnp.float32)
    upper = diffusion * keep[None, :]
    lower = jnp.concatenate([jnp.zeros((species, 1), jnp.float32), upper[:, :-1]], 1)
    rows = pl.pallas_call(
        thomas_kernel,
        out_shape=jax.ShapeDtypeStruct((depth, species, depth), jnp.float32),
        in_specs=[pl.BlockSpec(memory_space=pltpu.SMEM)],
        scratch_shapes=[pltpu.VMEM((depth, species, depth), jnp.float32)] * 2,
        cost_estimate=pl.CostEstimate(
            flops=12 * depth * species * depth,
            transcendentals=0,
            bytes_accessed=4 * 2 * depth * species * depth,
        ),
    )(diffusion)
    inverse = jnp.transpose(rows, (1, 0, 2))
    return (inverse, upper, lower)


def vertical_apply(w, upper, lower):
    zero_col = jnp.zeros(w.shape[:-1] + (1,), jnp.float32)
    beneath = jnp.concatenate([zero_col, w[..., :-1]], -1)
    overhead = jnp.concatenate([w[..., 1:], zero_col], -1)
    lo = lower[:, None, None, :]
    up = upper[:, None, None, :]
    return (lo + up) * w - lo * beneath - up * overhead


def slab_of(corr, tile, depth):
    return jnp.where(tile % 2 == 0, corr, depth - 1 - corr)


def x_ring():
    depth, tiles = lax.axis_size("corr"), lax.axis_size("tx")
    order = []
    for tile in range(tiles):
        for q in range(depth):
            corr = q if tile % 2 == 0 else depth - 1 - q
            order.append(corr * tiles + tile)
    return order


def ring_halo(block, axes, order, dim, width):
    size = len(order)
    length = block.shape[dim]
    up = [(order[g], order[(g + 1) % size]) for g in range(size)]
    down = [(j, i) for i, j in up]
    last = lax.slice_in_dim(block, length - width, length, axis=dim)
    first = lax.slice_in_dim(block, 0, width, axis=dim)
    if size == 2:
        got = lax.ppermute(jnp.concatenate([first, last], dim), axes, up)
        after = lax.slice_in_dim(got, 0, width, axis=dim)
        before = lax.slice_in_dim(got, width, 2 * width, axis=dim)
        return before, after
    before = lax.ppermute(last, axes, up)
    after = lax.ppermute(first, axes, down)
    return before, after


def swap_halo(block, axes, order, parity, dim, width):
    size = len(order)
    length = block.shape[dim]
    last = lax.slice_in_dim(block, length - width, length, axis=dim)
    first = lax.slice_in_dim(block, 0, width, axis=dim)
    got = []
    for offset in range(2):
        pairs = []
        for g in range(offset, size, 2):
            pairs += [(order[g], order[(g + 1) % size]), (order[(g + 1) % size], order[g])]
        sent = jnp.where(parity == offset, last, first)
        got.append(lax.ppermute(sent, axes, pairs))
    before = jnp.where(parity == 0, got[1], got[0])
    after = jnp.where(parity == 0, got[0], got[1])
    return before, after


def tendency(state, wind, parity):
    ring = x_ring()
    if len(ring) % 2 == 0:
        west, east = swap_halo(state, ("corr", "tx"), ring, parity, 2, 2)
    else:
        west, east = ring_halo(state, ("corr", "tx"), ring, 2, 2)
    south, north = ring_halo(state, ("ty",), list(range(lax.axis_size("ty"))), 3, 2)
    px = jnp.concatenate([west, state, east], 2)
    py = jnp.concatenate([south, state, north], 3)
    center = state
    twelfth = 1.0 / 12.0
    far_x = px[:, :, :-4] - px[:, :, 4:]
    near_x = px[:, :, 3:-1] - px[:, :, 1:-3]
    far_sum_x = px[:, :, :-4] + px[:, :, 4:]
    near_sum_x = px[:, :, 3:-1] + px[:, :, 1:-3]
    far_y = py[:, :, :, :-4] - py[:, :, :, 4:]
    near_y = py[:, :, :, 3:-1] - py[:, :, :, 1:-3]
    far_sum_y = py[:, :, :, :-4] + py[:, :, :, 4:]
    near_sum_y = py[:, :, :, 3:-1] + py[:, :, :, 1:-3]
    dx1 = (far_x + 8.0 * near_x) * twelfth
    dy1 = (far_y + 8.0 * near_y) * twelfth
    laplace = (
        16.0 * (near_sum_x + near_sum_y) - (far_sum_x + far_sum_y) - 60.0 * center
    ) * twelfth
    kappa = jnp.array([0.5, 1.0], jnp.float32)[None, :, None, None, None]
    first = center[:, 0]
    second = center[:, 1]
    square_term = first * first * second
    react = jnp.stack(
        [A_RATE - (B_RATE + 1.0) * first + square_term, B_RATE * first - square_term], 1
    )
    flow = -(wind[0][None, None] * dx1 + wind[1][None, None] * dy1)
    return DT * (flow + kappa * laplace + react)


def column_solve(rhs, inverse):
    return jnp.einsum(
        "lsxyk,sjk->lsxyj", rhs, inverse, precision=lax.Precision.HIGHEST
    )


def on_device(fields, wind, diffusion):
    inverse, upper, lower = vertical(diffusion)
    table = quad_cycle(STEPS)
    depth = lax.axis_size("corr")
    slab = fields.shape[1] // depth
    me = lax.axis_index("corr")
    tile = lax.axis_index("tx")
    start = slab_of(me, tile, depth) * slab
    parity = (tile * depth + slab_of(me, tile, depth)) % 2
    own_fields = lax.dynamic_slice_in_dim(fields, start, slab, 1)
    own_wind = lax.dynamic_slice_in_dim(wind, start, slab, 1)

    states = [own_fields] * depth
    e_hist = [dict() for _ in range(depth)]
    d_hist = [dict() for _ in range(depth)]
    g_now = [None] * depth
    for k in range(STEPS + depth - 1):
        active = [
            l for l in range(depth)
            if 0 <= k - l < STEPS or (k - l == STEPS and l < depth - 1)
        ]
        stacked = jnp.stack([states[l] for l in active], 0)
        own_e = tendency(stacked, own_wind, parity)
        feeds = [l for l in active if l < depth - 1]
        if feeds:
            lows = [active.index(l) for l in feeds]
            lo, hi = lows[0], lows[-1] + 1
            own_g = vertical_apply(stacked[lo:hi], upper, lower)
            for i, l in enumerate(feeds):
                m = k - l
                g_now[l] = own_g[i]
                d_hist[l][m] = own_e[lo + i] - own_g[i]
        moving = [l for l in active if k - l < STEPS]
        rhs = []
        for l in moving:
            m = k - l
            i = active.index(l)
            e_hist[l][m] = own_e[i]
            total = states[l]
            if l > 0:
                last = float(table[m, 4])
                quad = (1.0 - last) * g_now[l - 1] - e_hist[l - 1][m]
                for slot in range(4):
                    node = m - 3 + slot
                    if node >= 0:
                        quad = quad + float(table[m, slot]) * d_hist[l - 1][node]
                total = (total + quad) + last * own_e[active.index(l - 1)]
            rhs.append(total + own_e[i])
        solved = column_solve(jnp.stack(rhs, 0), inverse)
        for i, l in enumerate(moving):
            states[l] = solved[i]
    out = jnp.zeros((1,) + own_fields.shape[:1] + fields.shape[1:], jnp.float32)
    out = lax.dynamic_update_slice_in_dim(
        out, jnp.stack(states, 0)[me][None], start, 2
    )
    for shift in range(1, depth):
        origin = (me - shift) % depth
        got = None
        for level in range(depth):
            pairs = [((level + shift) % depth, level)]
            arrived = lax.ppermute(states[level][None], "corr", pairs)
            got = arrived if got is None else jnp.where(me == level, arrived, got)
        out = lax.dynamic_update_slice_in_dim(
            out, got, slab_of(origin, tile, depth) * slab, 2
        )
    return out


def solution(mesh):
    placed = (P(None, "tx", "ty", None), P(None, "tx", "ty", None), P())
    return jax.shard_map(
        on_device,
        mesh=mesh,
        in_specs=placed,
        out_specs=P("corr", None, "tx", "ty", None),
        check_vma=False,
    )
```

```python
import jax
import jax.numpy as jnp
import numpy as np
from jax import lax
from jax.experimental import pallas as pl
from jax.experimental.pallas import tpu as pltpu
from jax.sharding import PartitionSpec as P

STEPS = 8


DT = 0.1
A_RATE = 1.0
B_RATE = 3.0


def quad_cycle(count):
    table = np.zeros((count, 5))
    for m in range(count):
        first = max(0, m - 3)
        nodes = [float(j - m) for j in range(first, m + 2)]
        for i, xi in enumerate(nodes):
            coeffs = [1.0]
            for xo in nodes:
                if xo != xi:
                    widened = [0.0] * (len(coeffs) + 1)
                    for k, c in enumerate(coeffs):
                        widened[k] = widened[k] - xo * c / (xi - xo)
                        widened[k + 1] = widened[k + 1] + c / (xi - xo)
                    coeffs = widened
            integral = 0.0
            for k, c in enumerate(coeffs):
                integral = integral + c / (k + 1)
            table[m, first + i - (m - 3)] = integral
    return table


def thomas_kernel(diff_ref, out_ref, c_ref, d_ref):
    n = out_ref.shape[0]
    shape = out_ref.shape[1:]
    lanes = lax.broadcasted_iota(jnp.int32, shape, 1)
    species = lax.broadcasted_iota(jnp.int32, shape, 0)
    zero = jnp.zeros(shape, jnp.float32)

    def column(j):
        value = jnp.full(shape, diff_ref[0, j], jnp.float32)
        for s in range(1, shape[0]):
            value = jnp.where(species == s, diff_ref[s, j], value)
        return value

    def forward(j, carry):
        cprev, dprev = carry
        up = jnp.where(j < n - 1, column(j), 0.0)
        low = jnp.where(j > 0, column(jnp.maximum(j - 1, 0)), 0.0)
        inv = 1.0 / ((1.0 + low + up) + low * cprev)
        c = -up * inv
        d = (jnp.where(lanes == j, 1.0, 0.0) + low * dprev) * inv
        c_ref[j] = c
        d_ref[j] = d
        return c, d

    lax.fori_loop(0, n, forward, (zero, zero), unroll=16)

    def backward(i, x):
        j = n - 1 - i
        x = d_ref[j] - c_ref[j] * x
        out_ref[j] = x
        return x

    lax.fori_loop(0, n, backward, zero, unroll=16)


def vertical(diffusion):
    species, depth = diffusion.shape
    keep = (jnp.arange(depth) < depth - 1).astype(jnp.float32)
    upper = diffusion * keep[None, :]
    lower = jnp.concatenate([jnp.zeros((species, 1), jnp.float32), upper[:, :-1]], 1)
    rows = pl.pallas_call(
        thomas_kernel,
        out_shape=jax.ShapeDtypeStruct((depth, species, depth), jnp.float32),
        in_specs=[pl.BlockSpec(memory_space=pltpu.SMEM)],
        scratch_shapes=[pltpu.VMEM((depth, species, depth), jnp.float32)] * 2,
        cost_estimate=pl.CostEstimate(
            flops=12 * depth * species * depth,
            transcendentals=0,
            bytes_accessed=4 * 2 * depth * species * depth,
        ),
    )(diffusion)
    inverse = jnp.transpose(rows, (1, 0, 2))
    return (inverse, upper, lower)


def vertical_apply(w, upper, lower):
    zero_col = jnp.zeros(w.shape[:-1] + (1,), jnp.float32)
    beneath = jnp.concatenate([zero_col, w[..., :-1]], -1)
    overhead = jnp.concatenate([w[..., 1:], zero_col], -1)
    lo = lower[:, None, None, :]
    up = upper[:, None, None, :]
    return (lo + up) * w - lo * beneath - up * overhead


def slab_of(corr, tile, depth):
    return jnp.where(tile % 2 == 0, corr, depth - 1 - corr)


def x_ring():
    depth, tiles = lax.axis_size("corr"), lax.axis_size("tx")
    order = []
    for tile in range(tiles):
        for q in range(depth):
            corr = q if tile % 2 == 0 else depth - 1 - q
            order.append(corr * tiles + tile)
    return order


def ring_halo(block, axes, order, dim, width):
    size = len(order)
    length = block.shape[dim]
    up = [(order[g], order[(g + 1) % size]) for g in range(size)]
    down = [(j, i) for i, j in up]
    last = lax.slice_in_dim(block, length - width, length, axis=dim)
    first = lax.slice_in_dim(block, 0, width, axis=dim)
    if size == 2:
        got = lax.ppermute(jnp.concatenate([first, last], dim), axes, up)
        after = lax.slice_in_dim(got, 0, width, axis=dim)
        before = lax.slice_in_dim(got, width, 2 * width, axis=dim)
        return before, after
    before = lax.ppermute(last, axes, up)
    after = lax.ppermute(first, axes, down)
    return before, after


def swap_halo(block, axes, order, parity, dim, width):
    size = len(order)
    length = block.shape[dim]
    got = []
    for offset in range(2):
        pairs = []
        for g in range(offset, size, 2):
            pairs += [(order[g], order[(g + 1) % size]), (order[(g + 1) % size], order[g])]
        edge = jnp.where(parity == offset, length - width, 0)
        sent = lax.dynamic_slice_in_dim(block, edge, width, dim)
        got.append(lax.ppermute(sent, axes, pairs))
    before = jnp.where(parity == 0, got[1], got[0])
    after = jnp.where(parity == 0, got[0], got[1])
    return before, after


def tendency(state, wind, parity):
    ring = x_ring()
    if len(ring) % 2 == 0:
        west, east = swap_halo(state, ("corr", "tx"), ring, parity, 2, 2)
    else:
        west, east = ring_halo(state, ("corr", "tx"), ring, 2, 2)
    south, north = ring_halo(state, ("ty",), list(range(lax.axis_size("ty"))), 3, 2)
    px = jnp.concatenate([west, state, east], 2)
    py = jnp.concatenate([south, state, north], 3)
    center = state
    twelfth = 1.0 / 12.0
    far_x = px[:, :, :-4] - px[:, :, 4:]
    near_x = px[:, :, 3:-1] - px[:, :, 1:-3]
    far_sum_x = px[:, :, :-4] + px[:, :, 4:]
    near_sum_x = px[:, :, 3:-1] + px[:, :, 1:-3]
    far_y = py[:, :, :, :-4] - py[:, :, :, 4:]
    near_y = py[:, :, :, 3:-1] - py[:, :, :, 1:-3]
    far_sum_y = py[:, :, :, :-4] + py[:, :, :, 4:]
    near_sum_y = py[:, :, :, 3:-1] + py[:, :, :, 1:-3]
    dx1 = (far_x + 8.0 * near_x) * twelfth
    dy1 = (far_y + 8.0 * near_y) * twelfth
    laplace = (
        16.0 * (near_sum_x + near_sum_y) - (far_sum_x + far_sum_y) - 60.0 * center
    ) * twelfth
    kappa = jnp.array([0.5, 1.0], jnp.float32)[None, :, None, None, None]
    first = center[:, 0]
    second = center[:, 1]
    square_term = first * first * second
    react = jnp.stack(
        [A_RATE - (B_RATE + 1.0) * first + square_term, B_RATE * first - square_term], 1
    )
    flow = -(wind[0][None, None] * dx1 + wind[1][None, None] * dy1)
    return DT * (flow + kappa * laplace + react)


def column_solve(rhs, inverse):
    return jnp.einsum(
        "lsxyk,sjk->lsxyj", rhs, inverse, precision=lax.Precision.HIGHEST
    )


def on_device(fields, wind, diffusion):
    inverse, upper, lower = vertical(diffusion)
    table = quad_cycle(STEPS)
    depth = lax.axis_size("corr")
    slab = fields.shape[1] // depth
    me = lax.axis_index("corr")
    tile = lax.axis_index("tx")
    start = slab_of(me, tile, depth) * slab
    parity = (tile * depth + slab_of(me, tile, depth)) % 2
    own_fields = lax.dynamic_slice_in_dim(fields, start, slab, 1)
    own_wind = lax.dynamic_slice_in_dim(wind, start, slab, 1)

    states = [own_fields] * depth
    e_hist = [dict() for _ in range(depth)]
    d_hist = [dict() for _ in range(depth)]
    g_now = [None] * depth
    for k in range(STEPS + depth - 1):
        active = [
            l for l in range(depth)
            if 0 <= k - l < STEPS or (k - l == STEPS and l < depth - 1)
        ]
        stacked = jnp.stack([states[l] for l in active], 0)
        own_e = tendency(stacked, own_wind, parity)
        feeds = [l for l in active if l < depth - 1]
        if feeds:
            lows = [active.index(l) for l in feeds]
            lo, hi = lows[0], lows[-1] + 1
            own_g = vertical_apply(stacked[lo:hi], upper, lower)
            for i, l in enumerate(feeds):
                m = k - l
                g_now[l] = own_g[i]
                d_hist[l][m] = own_e[lo + i] - own_g[i]
        moving = [l for l in active if k - l < STEPS]
        rhs = []
        for l in moving:
            m = k - l
            i = active.index(l)
            e_hist[l][m] = own_e[i]
            total = states[l] + own_e[i]
            if l > 0:
                quad = None
                for slot in range(5):
                    node = m - 3 + slot
                    if node >= 0:
                        term = float(table[m, slot]) * d_hist[l - 1][node]
                        quad = term if quad is None else quad + term
                total = total + (quad + g_now[l - 1] - e_hist[l - 1][m])
            rhs.append(total)
        solved = column_solve(jnp.stack(rhs, 0), inverse)
        for i, l in enumerate(moving):
            states[l] = solved[i]
    out = jnp.zeros((1,) + own_fields.shape[:1] + fields.shape[1:], jnp.float32)
    out = lax.dynamic_update_slice_in_dim(
        out, jnp.stack(states, 0)[me][None], start, 2
    )
    for shift in range(1, depth):
        origin = (me - shift) % depth
        got = None
        for level in range(depth):
            pairs = [((level + shift) % depth, level)]
            arrived = lax.ppermute(states[level][None], "corr", pairs)
            got = arrived if got is None else jnp.where(me == level, arrived, got)
        out = lax.dynamic_update_slice_in_dim(
            out, got, slab_of(origin, tile, depth) * slab, 2
        )
    return out


def solution(mesh):
    placed = (P(None, "tx", "ty", None), P(None, "tx", "ty", None), P())
    return jax.shard_map(
        on_device,
        mesh=mesh,
        in_specs=placed,
        out_specs=P("corr", None, "tx", "ty", None),
        check_vma=False,
    )
```

```python
import jax
import jax.numpy as jnp
import numpy as np
from jax import lax
from jax.experimental import pallas as pl
from jax.experimental.pallas import tpu as pltpu
from jax.sharding import PartitionSpec as P

STEPS = 8


DT = 0.1
A_RATE = 1.0
B_RATE = 3.0


def quad_cycle(count):
    table = np.zeros((count, 5))
    for m in range(count):
        first = max(0, m - 3)
        nodes = [float(j - m) for j in range(first, m + 2)]
        for i, xi in enumerate(nodes):
            coeffs = [1.0]
            for xo in nodes:
                if xo != xi:
                    widened = [0.0] * (len(coeffs) + 1)
                    for k, c in enumerate(coeffs):
                        widened[k] = widened[k] - xo * c / (xi - xo)
                        widened[k + 1] = widened[k + 1] + c / (xi - xo)
                    coeffs = widened
            integral = 0.0
            for k, c in enumerate(coeffs):
                integral = integral + c / (k + 1)
            table[m, first + i - (m - 3)] = integral
    return table


def thomas_kernel(diff_ref, out_ref, c_ref, d_ref):
    n = out_ref.shape[0]
    shape = out_ref.shape[1:]
    lanes = lax.broadcasted_iota(jnp.int32, shape, 1)
    species = lax.broadcasted_iota(jnp.int32, shape, 0)
    zero = jnp.zeros(shape, jnp.float32)

    def column(j):
        value = jnp.full(shape, diff_ref[0, j], jnp.float32)
        for s in range(1, shape[0]):
            value = jnp.where(species == s, diff_ref[s, j], value)
        return value

    def forward(j, carry):
        cprev, dprev = carry
        up = jnp.where(j < n - 1, column(j), 0.0)
        low = jnp.where(j > 0, column(jnp.maximum(j - 1, 0)), 0.0)
        inv = 1.0 / ((1.0 + low + up) + low * cprev)
        c = -up * inv
        d = (jnp.where(lanes == j, 1.0, 0.0) + low * dprev) * inv
        c_ref[j] = c
        d_ref[j] = d
        return c, d

    lax.fori_loop(0, n, forward, (zero, zero), unroll=16)

    def backward(i, x):
        j = n - 1 - i
        x = d_ref[j] - c_ref[j] * x
        out_ref[j] = x
        return x

    lax.fori_loop(0, n, backward, zero, unroll=16)


def vertical(diffusion):
    species, depth = diffusion.shape
    keep = (jnp.arange(depth) < depth - 1).astype(jnp.float32)
    upper = diffusion * keep[None, :]
    lower = jnp.concatenate([jnp.zeros((species, 1), jnp.float32), upper[:, :-1]], 1)
    rows = pl.pallas_call(
        thomas_kernel,
        out_shape=jax.ShapeDtypeStruct((depth, species, depth), jnp.float32),
        in_specs=[pl.BlockSpec(memory_space=pltpu.SMEM)],
        scratch_shapes=[pltpu.VMEM((depth, species, depth), jnp.float32)] * 2,
        cost_estimate=pl.CostEstimate(
            flops=12 * depth * species * depth,
            transcendentals=0,
            bytes_accessed=4 * 2 * depth * species * depth,
        ),
    )(diffusion)
    inverse = jnp.transpose(rows, (1, 0, 2))
    return (inverse, upper, lower)


def vertical_apply(w, upper, lower):
    zero_col = jnp.zeros(w.shape[:-1] + (1,), jnp.float32)
    beneath = jnp.concatenate([zero_col, w[..., :-1]], -1)
    overhead = jnp.concatenate([w[..., 1:], zero_col], -1)
    lo = lower[:, None, None, :]
    up = upper[:, None, None, :]
    return (lo + up) * w - lo * beneath - up * overhead


def slab_of(corr, tile, depth):
    return jnp.where(tile % 2 == 0, corr, depth - 1 - corr)


def x_ring():
    depth, tiles = lax.axis_size("corr"), lax.axis_size("tx")
    order = []
    for tile in range(tiles):
        for q in range(depth):
            corr = q if tile % 2 == 0 else depth - 1 - q
            order.append(corr * tiles + tile)
    return order


def ring_halo(block, axes, order, dim, width):
    size = len(order)
    length = block.shape[dim]
    up = [(order[g], order[(g + 1) % size]) for g in range(size)]
    down = [(j, i) for i, j in up]
    last = lax.slice_in_dim(block, length - width, length, axis=dim)
    first = lax.slice_in_dim(block, 0, width, axis=dim)
    if size == 2:
        got = lax.ppermute(jnp.stack([first, last], 0), axes, up)
        return got[1], got[0]
    before = lax.ppermute(last, axes, up)
    after = lax.ppermute(first, axes, down)
    return before, after


def swap_halo(block, axes, order, parity, dim, width):
    size = len(order)
    length = block.shape[dim]
    last = lax.slice_in_dim(block, length - width, length, axis=dim)
    first = lax.slice_in_dim(block, 0, width, axis=dim)
    got = []
    for offset in range(2):
        pairs = []
        for g in range(offset, size, 2):
            pairs += [(order[g], order[(g + 1) % size]), (order[(g + 1) % size], order[g])]
        sent = jnp.where(parity == offset, last, first)
        got.append(lax.ppermute(sent, axes, pairs))
    before = jnp.where(parity == 0, got[1], got[0])
    after = jnp.where(parity == 0, got[0], got[1])
    return before, after


def tendency(state, wind, parity):
    ring = x_ring()
    if len(ring) % 2 == 0:
        west, east = swap_halo(state, ("corr", "tx"), ring, parity, 2, 2)
    else:
        west, east = ring_halo(state, ("corr", "tx"), ring, 2, 2)
    south, north = ring_halo(state, ("ty",), list(range(lax.axis_size("ty"))), 3, 2)
    px = jnp.concatenate([west, state, east], 2)
    py = jnp.concatenate([south, state, north], 3)
    center = state
    twelfth = 1.0 / 12.0
    far_x = px[:, :, :-4] - px[:, :, 4:]
    near_x = px[:, :, 3:-1] - px[:, :, 1:-3]
    far_sum_x = px[:, :, :-4] + px[:, :, 4:]
    near_sum_x = px[:, :, 3:-1] + px[:, :, 1:-3]
    far_y = py[:, :, :, :-4] - py[:, :, :, 4:]
    near_y = py[:, :, :, 3:-1] - py[:, :, :, 1:-3]
    far_sum_y = py[:, :, :, :-4] + py[:, :, :, 4:]
    near_sum_y = py[:, :, :, 3:-1] + py[:, :, :, 1:-3]
    dx1 = (far_x + 8.0 * near_x) * twelfth
    dy1 = (far_y + 8.0 * near_y) * twelfth
    laplace = (
        16.0 * (near_sum_x + near_sum_y) - (far_sum_x + far_sum_y) - 60.0 * center
    ) * twelfth
    kappa = jnp.array([0.5, 1.0], jnp.float32)[None, :, None, None, None]
    first = center[:, 0]
    second = center[:, 1]
    square_term = first * first * second
    react = jnp.stack(
        [A_RATE - (B_RATE + 1.0) * first + square_term, B_RATE * first - square_term], 1
    )
    flow = -(wind[0][None, None] * dx1 + wind[1][None, None] * dy1)
    return DT * (flow + kappa * laplace + react)


def column_solve(rhs, inverse):
    return jnp.einsum(
        "lsxyk,sjk->lsxyj", rhs, inverse, precision=lax.Precision.HIGHEST
    )


def on_device(fields, wind, diffusion):
    inverse, upper, lower = vertical(diffusion)
    table = quad_cycle(STEPS)
    depth = lax.axis_size("corr")
    slab = fields.shape[1] // depth
    me = lax.axis_index("corr")
    tile = lax.axis_index("tx")
    start = slab_of(me, tile, depth) * slab
    parity = (tile * depth + slab_of(me, tile, depth)) % 2
    own_fields = lax.dynamic_slice_in_dim(fields, start, slab, 1)
    own_wind = lax.dynamic_slice_in_dim(wind, start, slab, 1)

    states = [own_fields] * depth
    e_hist = [dict() for _ in range(depth)]
    d_hist = [dict() for _ in range(depth)]
    g_now = [None] * depth
    for k in range(STEPS + depth - 1):
        active = [
            l for l in range(depth)
            if 0 <= k - l < STEPS or (k - l == STEPS and l < depth - 1)
        ]
        stacked = jnp.stack([states[l] for l in active], 0)
        own_e = tendency(stacked, own_wind, parity)
        feeds = [l for l in active if l < depth - 1]
        if feeds:
            lows = [active.index(l) for l in feeds]
            lo, hi = lows[0], lows[-1] + 1
            own_g = vertical_apply(stacked[lo:hi], upper, lower)
            for i, l in enumerate(feeds):
                m = k - l
                g_now[l] = own_g[i]
                d_hist[l][m] = own_e[lo + i] - own_g[i]
        moving = [l for l in active if k - l < STEPS]
        rhs = []
        for l in moving:
            m = k - l
            i = active.index(l)
            e_hist[l][m] = own_e[i]
            total = states[l] + own_e[i]
            if l > 0:
                quad = None
                for slot in range(5):
                    node = m - 3 + slot
                    if node >= 0:
                        term = float(table[m, slot]) * d_hist[l - 1][node]
                        quad = term if quad is None else quad + term
                total = total + (quad + g_now[l - 1] - e_hist[l - 1][m])
            rhs.append(total)
        solved = column_solve(jnp.stack(rhs, 0), inverse)
        for i, l in enumerate(moving):
            states[l] = solved[i]
    out = jnp.zeros((1,) + own_fields.shape[:1] + fields.shape[1:], jnp.float32)
    out = lax.dynamic_update_slice_in_dim(
        out, jnp.stack(states, 0)[me][None], start, 2
    )
    for shift in range(1, depth):
        origin = (me - shift) % depth
        got = None
        for level in range(depth):
            pairs = [((level + shift) % depth, level)]
            arrived = lax.ppermute(states[level][None], "corr", pairs)
            got = arrived if got is None else jnp.where(me == level, arrived, got)
        out = lax.dynamic_update_slice_in_dim(
            out, got, slab_of(origin, tile, depth) * slab, 2
        )
    return out


def solution(mesh):
    placed = (P(None, "tx", "ty", None), P(None, "tx", "ty", None), P())
    return jax.shard_map(
        on_device,
        mesh=mesh,
        in_specs=placed,
        out_specs=P("corr", None, "tx", "ty", None),
        check_vma=False,
    )
```
